512 devices in a mesh: rep: 8 (over y), tp: 64 (over z, x, core).
Axes of the slice: x: 4, y: 8, z: 8, core: 2. Of those that a mesh axis runs over, the one named last changes fastest.
Arguments:
- hidden: float32 [256, 2304], P('rep', 'tp'), parts along dimension 0
- attn_gain: float32 [2304], P('tp'), may hold values from 0.5 to 1.5
- w_qkv: bfloat16 [2304, 6912], P('tp'), may hold values from -0.125 to 0.125
- w_out: bfloat16 [2304, 2304], P(None, 'tp'), may hold values from -0.125 to 0.125
- prefix_keys: bfloat16 [24, 2048, 2304], P('rep', 'tp'), parts along dimension 0
- prefix_values: bfloat16 [24, 2048, 2304], P('rep', 'tp'), parts along dimension 0, may hold values from -6 to 6
- private_keys: bfloat16 [64, 512, 2304], P('rep', 'tp'), parts along dimension 0, may hold values from -15 to 15
- private_values: bfloat16 [64, 512, 2304], P('rep', 'tp'), parts along dimension 0, may hold values from -6 to 6
- group_ids: int32 [64], P('rep'), parts along dimension 0, may hold values from 0 to 2
- private_lengths: int32 [64], P('rep'), parts along dimension 0, may hold values from 1 to 512, as said below
- moe_gain: float32 [2304], replicated, may hold values from 0.5 to 1.5
- router: bfloat16 [2304, 4], replicated, may hold values from -0.25 to 0.25
- w_gate: bfloat16 [2304, 11520], P(None, 'tp'), may hold values from -0.125 to 0.125
- w_up: bfloat16 [2304, 11520], P(None, 'tp'), may hold values from -0.125 to 0.125
- w_down: bfloat16 [11520, 2304], P('tp'), may hold values from -0.3125 to 0.3125
- routes: int32 [256, 2], P('rep'), parts along dimension 0, may hold values from 0 to 3, all different within a row
Outputs:
- mixed: float32 [256, 2304], P('rep', 'tp'), parts along dimension 0
The draws below stay inside these ranges and needn't reach their ends.
There are 8 independent parts, one for each index of `rep`. The reference program is written for one: setup_inputs(seed, part) draws one part's arguments, and reference() takes and returns one part's arrays. A program takes and returns all parts, laid end to end along the dimension named above; an argument that names none is the same for every part. Nothing has to cross between parts.
Inputs may be any that keep to these rules, and one draw needn't show every extreme that they name: `private_lengths`: some request of every draw has all 512 positions live. `routes`: the two experts of a token differ.
All inputs are finite; a program needn't handle non-finite values.
Results may differ from the reference program's by a relative error of at most 0.0083.
Values may be sent and summed in bfloat16 or wider, within the bound.
No kernel may reach another device: no remote copies, remote signals or barrier semaphores. Data moves between devices by JAX's collectives and lax.ppermute only.
A program may use at most 128 MiB of HBM per device.

```python
import jax
import jax.numpy as jnp
from jax import lax

D = 2304
HEADS = 36
HDIM = 64
EXPERTS = 4
FF = 2880
NEW = 4
REQ = 8
GROUPS = 3
TOKENS = 32
PLEN = 2048
PRIV = 512


def draw_hidden(key, part):
    base_draw = jnp.clip(jax.random.normal(key, (TOKENS, D), jnp.float32), -6.0, 6.0)
    columns = jnp.arange(D, dtype=jnp.float32) / D
    roughness = jax.random.uniform(jax.random.fold_in(key, 1), (1, D), jnp.float32, 0.5, 1.5)
    result = base_draw * (3.0 ** (columns - 0.5))[None, :] * roughness
    return result


def draw_prefix_keys(key, part):
    base_draw = 3.0 * jnp.clip(jax.random.normal(key, (GROUPS, PLEN, D), jnp.float32), -6.0, 6.0)
    return base_draw.astype(jnp.bfloat16)


def draw_private_lengths(key, part):
    drawn = jax.random.randint(key, (REQ,), 1, PRIV + 1)
    chosen = jax.random.randint(jax.random.fold_in(key, 1), (), 0, REQ)
    return jnp.where(jnp.arange(REQ) == chosen, PRIV, drawn).astype(jnp.int32)


def with_ends(values, key, smallest, top_value):
    extent = values.shape
    spot = [jax.random.randint(jax.random.fold_in(key, axis), (), 0, extent[axis]) for axis in range(len(extent))]
    values = values.at[tuple(spot)].set(smallest)
    longest = extent.index(max(extent))
    spot[longest] = (spot[longest] + 1) % extent[longest]
    return values.at[tuple(spot)].set(top_value)


def spiked(values, own_key, source, target, parts, factor):
    def block_of(position):
        return (jnp.arange(values.shape[position]) // (values.shape[position] // parts)).reshape((-1,) + (1,) * (values.ndim - 1 - position))

    near = jax.random.permutation(own_key, parts)[block_of(target)]
    far = (block_of(target) + parts // 2) % parts
    return jnp.where((block_of(source) == near) | (block_of(source) == far), factor * values, values)


def block_scale(own_key, shape, shards, low, largest):
    factor_of, own = 1.0, jax.random.fold_in(own_key, 6)
    for axis_at, parts in shards:
        heights = jnp.exp(jax.random.uniform(jax.random.fold_in(own, axis_at), (parts,), jnp.float32, low / len(shards), largest / len(shards)))
        factor_of = factor_of * jnp.repeat(heights, shape[axis_at] // parts).reshape([-1 if axis == axis_at else 1 for axis in range(len(shape))])
    return factor_of


def choose_distinct(own_key, rows, amount, top, lift):
    sequence = jax.random.permutation(jax.random.fold_in(own_key, 1), amount)
    pull = sequence
    for power in range(3):
        pull = pull * pull // amount
    pull = pull * lift // amount
    chance = jax.random.randint(jax.random.fold_in(own_key, 2), (rows, amount), 0, 4096) + pull
    holders = jax.random.permutation(jax.random.fold_in(own_key, 3), rows)[jnp.arange(amount) % rows]
    chance = jnp.where(jnp.arange(rows)[:, None] == holders[None, :], 1 << 14, chance)
    priority = chance * amount + jnp.arange(amount)
    return lax.top_k(priority.astype(jnp.int32), top)[1].astype(jnp.int32)


def bell_draw(rng, shape, deviation, most, cuts=(), held_as=jnp.bfloat16):
    entries = jax.random.normal(rng, shape, jnp.float32) * deviation
    if len(cuts) > 0:
        entries = block_scale(rng, shape, cuts, -0.22, 0.18) * entries
    return jnp.clip(entries, min=-most, max=most).astype(held_as)


def noise_with(key, dims, scale, bound, cuts, heavy, kind=jnp.bfloat16):
    entries = scale * jax.random.normal(key, dims, jnp.float32)
    if cuts:
        entries = entries * block_scale(key, dims, cuts, -0.22, 0.18)
    return jnp.clip(spiked(entries, jax.random.fold_in(key, 3), *heavy), -bound, bound).astype(kind)


def setup_inputs(seed: int = 0, part: int = 0) -> dict:
    key_of = jax.random.split(jax.random.key(seed), 17)
    own_keys = jax.random.split(jax.random.fold_in(key_of[16], part), 17)
    return {
        "hidden": draw_hidden(jax.random.fold_in(jax.random.fold_in(key_of[16], part), 71), part),
        "attn_gain": jnp.clip(1.0 + 0.1 * jax.random.normal(key_of[1], (D,), jnp.float32), 0.5, 1.5),
        "w_qkv": bell_draw(key_of[2], (D, 3 * D), D ** -0.5, 0.125, ((0, 64),)),
        "w_out": bell_draw(key_of[3], (D, D), D ** -0.5, 0.125, ((1, 64),)),
        "prefix_keys": draw_prefix_keys(jax.random.fold_in(jax.random.fold_in(key_of[16], part), 71), part),
        "prefix_values": bell_draw(own_keys[5], (GROUPS, PLEN, D), 1.0, 6.0, ((1, 64),)),
        "private_keys": bell_draw(own_keys[6], (REQ, PRIV, D), 3.0, 15.0, ((1, 64),)),
        "private_values": bell_draw(own_keys[7], (REQ, PRIV, D), 1.0, 6.0, ((1, 64),)),
        "group_ids": with_ends(jax.random.randint(own_keys[8], (REQ,), 0, GROUPS), jax.random.fold_in(own_keys[8], 1), 0, GROUPS - 1).astype(jnp.int32),
        "private_lengths": draw_private_lengths(jax.random.fold_in(jax.random.fold_in(key_of[16], part), 71), part),
        "moe_gain": jnp.clip(1.0 + 0.1 * jax.random.normal(key_of[10], (D,), jnp.float32), 0.5, 1.5),
        "router": bell_draw(key_of[11], (D, EXPERTS), (D // 4) ** -0.5, 0.25),
        "w_gate": bell_draw(key_of[12], (D, EXPERTS * FF), D ** -0.5, 0.125, ((1, 64),)),
        "w_up": bell_draw(key_of[13], (D, EXPERTS * FF), D ** -0.5, 0.125, ((1, 64),)),
        "w_down": noise_with(key_of[14], (EXPERTS * FF, D), FF ** -0.5, 0.3125, ((0, 64),), (0, 1, 64, 4.0)),
        "routes": choose_distinct(own_keys[15], TOKENS, EXPERTS, 2, 4096),
    }


EPSILON = 1e-05
BLOCKED = -1e+30

def rotate_heads(vectors, places):
    half_dim = HDIM // 2
    frequencies = 10000.0 ** (-jnp.arange(half_dim, dtype=jnp.float32) / half_dim)
    angles = places.astype(jnp.float32)[:, None] * frequencies[None, :]
    cosine = jnp.cos(angles)[:, None, :]
    sine_part = jnp.sin(angles)[:, None, :]
    first = vectors[..., :half_dim]
    second = vectors[..., half_dim:]
    return jnp.concatenate([first * cosine - second * sine_part, second * cosine + first * sine_part], axis=-1)

def reference(hidden, attn_gain, w_qkv, w_out, prefix_keys, prefix_values, private_keys, private_values, group_ids, private_lengths, moe_gain, router, w_gate, w_up, w_down, routes):
    model_width = D
    all_tokens = REQ * NEW
    score_scale = HDIM ** (-0.5)
    scaled = (hidden * attn_gain[None, :]).astype(jnp.bfloat16)
    inv_attn = lax.rsqrt(lax.optimization_barrier(jnp.sum(hidden * hidden, axis=1)) / model_width + EPSILON)
    qkv = (inv_attn[:, None] * jnp.dot(scaled, w_qkv, preferred_element_type=jnp.float32)).astype(jnp.bfloat16)
    own_lengths = jnp.broadcast_to(private_lengths[:, None], (REQ, NEW)).reshape(all_tokens)
    places = PLEN + own_lengths + jnp.arange(all_tokens, dtype=jnp.int32) % NEW
    queries = rotate_heads(qkv[:, :model_width].astype(jnp.float32).reshape(all_tokens, HEADS, HDIM), places).astype(jnp.bfloat16)
    fresh_keys = rotate_heads(qkv[:, model_width:2 * model_width].astype(jnp.float32).reshape(all_tokens, HEADS, HDIM), places).astype(jnp.bfloat16)
    fresh_values = qkv[:, 2 * model_width:].reshape(REQ, NEW, HEADS, HDIM)
    queries = queries.reshape(REQ, NEW, HEADS, HDIM)
    fresh_keys = fresh_keys.reshape(REQ, NEW, HEADS, HDIM)
    causal = jnp.arange(NEW)[:, None] >= jnp.arange(NEW)[None, :]

    def one_request(pieces):
        query_r, key_r, value_r, group_id, length, priv_keys, priv_values = pieces
        query_f = query_r.astype(jnp.float32)
        pre_keys = lax.dynamic_index_in_dim(prefix_keys, group_id, 0, keepdims=False).astype(jnp.float32).reshape(PLEN, HEADS, HDIM)
        pre_values = lax.dynamic_index_in_dim(prefix_values, group_id, 0, keepdims=False).astype(jnp.float32).reshape(PLEN, HEADS, HDIM)
        pre_scores = jnp.einsum('jhd,phd->jhp', query_f, pre_keys) * score_scale
        priv_scores = jnp.einsum('jhd,phd->jhp', query_f, priv_keys.astype(jnp.float32).reshape(PRIV, HEADS, HDIM)) * score_scale
        live = jnp.arange(PRIV, dtype=jnp.int32) < length
        priv_scores = jnp.where(live[None, None, :], priv_scores, BLOCKED)
        new_scores = jnp.einsum('jhd,ihd->jhi', query_f, key_r.astype(jnp.float32)) * score_scale
        new_scores = jnp.where(causal[:, None, :], new_scores, BLOCKED)
        joined = jnp.concatenate([pre_scores, priv_scores, new_scores], axis=-1)
        joint_peak = lax.optimization_barrier(jnp.max(joined, axis=-1, keepdims=True))
        weights = jnp.exp(joined - joint_peak)
        totals = lax.optimization_barrier(jnp.sum(weights, axis=-1))
        pre_part = jnp.einsum('jhp,phd->jhd', weights[..., :PLEN], pre_values)
        priv_part = jnp.einsum('jhp,phd->jhd', weights[..., PLEN:PLEN + PRIV], priv_values.astype(jnp.float32).reshape(PRIV, HEADS, HDIM))
        new_part = jnp.einsum('jhi,ihd->jhd', weights[..., PLEN + PRIV:], value_r.astype(jnp.float32))
        return (pre_part + priv_part + new_part) / totals[..., None]
    outputs = lax.map(one_request, (queries, fresh_keys, fresh_values, group_ids, private_lengths, private_keys, private_values))
    attended = outputs.reshape(all_tokens, model_width).astype(jnp.bfloat16)
    residual = hidden + jnp.dot(attended, w_out, preferred_element_type=jnp.float32)
    inv_norm = lax.rsqrt(lax.optimization_barrier(jnp.mean(residual * residual, axis=1)) + EPSILON)
    normed = (residual * inv_norm[:, None] * moe_gain[None, :]).astype(jnp.bfloat16)
    logits = jnp.dot(normed, router, preferred_element_type=jnp.float32)
    expert_ids = jnp.arange(EXPERTS, dtype=jnp.int32)
    first_pick = routes[:, 0:1] == expert_ids[None, :]
    second_pick = routes[:, 1:2] == expert_ids[None, :]
    first_logit = lax.optimization_barrier(jnp.sum(jnp.where(first_pick, logits, 0.0), axis=1))
    second_logit = lax.optimization_barrier(jnp.sum(jnp.where(second_pick, logits, 0.0), axis=1))
    first_weight = jax.nn.sigmoid(first_logit - second_logit)
    mix_coef = first_weight[:, None] * first_pick.astype(jnp.float32) + (1.0 - first_weight)[:, None] * second_pick.astype(jnp.float32)
    column_coef = jnp.repeat(mix_coef, FF, axis=1)
    gate_out = jnp.dot(normed, w_gate, preferred_element_type=jnp.float32)
    up_out = jnp.dot(normed, w_up, preferred_element_type=jnp.float32)
    inner_act = (jax.nn.silu(gate_out) * up_out * column_coef).astype(jnp.bfloat16)
    return residual + jnp.dot(inner_act, w_down, preferred_element_type=jnp.float32)
```

```python
import jax
import jax.numpy as jnp
from jax import lax
from jax.sharding import PartitionSpec as P

HEADS = 36
HDIM = 64
FF = 2880
NEW = 4


EPSILON = 1e-05
BLOCKED = -1e30


def rotate_heads(vectors, places):
    half_dim = HDIM // 2
    frequencies = 10000.0 ** (-jnp.arange(half_dim, dtype=jnp.float32) / half_dim)
    angles = places.astype(jnp.float32)[:, None] * frequencies[None, :]
    cosine = jnp.cos(angles)[:, None, :]
    sine_part = jnp.sin(angles)[:, None, :]
    first = vectors[..., :half_dim]
    second = vectors[..., half_dim:]
    return jnp.concatenate(
        [first * cosine - second * sine_part, second * cosine + first * sine_part], axis=-1
    )


def scale_rows(values, factor):
    row_count, head_count = factor.shape
    return (values.reshape(row_count, head_count, -1) * factor[..., None]).reshape(row_count, -1)


def partner_pairs(count, bit):
    return [(i, i ^ bit) for i in range(count)]


def tp_bits():
    count = lax.axis_size("tp")
    bits = []
    bit = count // 2
    while bit >= 1:
        bits.append(bit)
        bit //= 2
    return count, bits


def scatter_sum(values):
    count, bits = tp_bits()
    own_rank = lax.axis_index("tp")
    for bit in bits:
        half = values.shape[1] // 2
        side = (own_rank // bit) % 2
        keep = lax.dynamic_slice_in_dim(values, side * half, half, axis=1)
        send = lax.dynamic_slice_in_dim(values, (1 - side) * half, half, axis=1)
        values = keep + lax.ppermute(send, "tp", partner_pairs(count, bit))
    return values


def gather_cols(values):
    count, bits = tp_bits()
    own_rank = lax.axis_index("tp")
    for bit in reversed(bits):
        side = (own_rank // bit) % 2
        other = lax.ppermute(values, "tp", partner_pairs(count, bit))
        values = jnp.where(
            side == 0,
            jnp.concatenate([values, other], axis=1),
            jnp.concatenate([other, values], axis=1),
        )
    return values


def merge_softmax(peak, total, weighted):
    count, bits = tp_bits()
    heads = peak.shape[1]
    for bit in reversed(bits):
        packed = jnp.concatenate([peak, total, weighted], axis=1)
        other = lax.ppermute(packed, "tp", partner_pairs(count, bit))
        other_peak = other[:, :heads]
        other_total = other[:, heads : 2 * heads]
        other_weighted = other[:, 2 * heads :]
        joint = jnp.maximum(peak, other_peak)
        own_factor = jnp.exp(peak - joint)
        other_factor = jnp.exp(other_peak - joint)
        total = total * own_factor + other_total * other_factor
        weighted = scale_rows(weighted, own_factor) + scale_rows(other_weighted, other_factor)
        peak = joint
    return peak, total, weighted


def merge_parts(first, second):
    joint_peak = jnp.maximum(first[0], second[0])
    first_factor = jnp.exp(first[0] - joint_peak)
    second_factor = jnp.exp(second[0] - joint_peak)
    totals = first[1] * first_factor + second[1] * second_factor
    weighted = scale_rows(first[2], first_factor) + scale_rows(second[2], second_factor)
    return (joint_peak, totals, weighted)


def on_device(
    hidden,
    attn_gain,
    w_qkv,
    w_out,
    prefix_keys,
    prefix_values,
    private_keys,
    private_values,
    group_ids,
    private_lengths,
    moe_gain,
    router,
    w_gate,
    w_up,
    w_down,
    routes,
):
    model_width = w_out.shape[0]
    all_tokens = hidden.shape[0]
    requests = group_ids.shape[0]
    group_count = prefix_keys.shape[0]
    prefix_block = prefix_keys.shape[1]
    private_block = private_keys.shape[1]
    own_rank = lax.axis_index("tp")
    score_scale = HDIM ** (-0.5)
    scaled = (hidden * attn_gain[None, :]).astype(jnp.bfloat16)
    partial_qkv = jnp.dot(scaled, w_qkv, preferred_element_type=jnp.float32)
    own_squares = jnp.sum(hidden * hidden, axis=1)
    qkv_width = partial_qkv.shape[1]
    tp_count = lax.axis_size("tp")
    padded_width = -(-(qkv_width + 1) // tp_count) * tp_count
    packed = jnp.concatenate(
        [
            partial_qkv,
            own_squares[:, None],
            jnp.zeros((all_tokens, padded_width - qkv_width - 1), jnp.float32),
        ],
        axis=1,
    )
    packed = gather_cols(scatter_sum(packed))
    summed = packed[:, :qkv_width]
    squares = packed[:, qkv_width]
    inv_attn = lax.rsqrt(squares / model_width + EPSILON)
    qkv = (inv_attn[:, None] * summed).astype(jnp.bfloat16)
    own_lengths = jnp.broadcast_to(private_lengths[:, None], (requests, NEW)).reshape(all_tokens)
    places = (
        prefix_block * lax.axis_size("tp")
        + own_lengths
        + jnp.arange(all_tokens, dtype=jnp.int32) % NEW
    )
    queries = rotate_heads(
        qkv[:, :model_width].astype(jnp.float32).reshape(all_tokens, HEADS, HDIM), places
    ).astype(jnp.bfloat16)
    fresh_keys = rotate_heads(
        qkv[:, model_width : 2 * model_width].astype(jnp.float32).reshape(all_tokens, HEADS, HDIM),
        places,
    ).astype(jnp.bfloat16)
    fresh_values = qkv[:, 2 * model_width :].astype(jnp.float32).reshape(requests, NEW, HEADS, HDIM)
    query_f = queries.astype(jnp.float32).reshape(requests, NEW, HEADS, HDIM)
    pre_keys = prefix_keys.astype(jnp.float32).reshape(group_count, prefix_block, HEADS, HDIM)
    pre_scores = jnp.einsum("rjhd,gphd->rjhgp", query_f, pre_keys) * score_scale
    member = group_ids[:, None] == jnp.arange(group_count, dtype=jnp.int32)[None, :]
    pre_scores = jnp.where(member[:, None, None, :, None], pre_scores, BLOCKED)
    priv_keys = private_keys.astype(jnp.float32).reshape(requests, private_block, HEADS, HDIM)
    priv_scores = jnp.einsum("rjhd,rphd->rjhp", query_f, priv_keys) * score_scale
    slots = own_rank * private_block + jnp.arange(private_block, dtype=jnp.int32)
    live = slots[None, :] < private_lengths[:, None]
    priv_scores = jnp.where(live[:, None, None, :], priv_scores, BLOCKED)
    local_peak = jnp.maximum(jnp.max(pre_scores, axis=(3, 4)), jnp.max(priv_scores, axis=3))
    pre_weights = jnp.exp(pre_scores - local_peak[..., None, None])
    priv_weights = jnp.exp(priv_scores - local_peak[..., None])
    local_total = jnp.sum(pre_weights, axis=(3, 4)) + jnp.sum(priv_weights, axis=3)
    pre_vals = prefix_values.astype(jnp.float32).reshape(group_count, prefix_block, HEADS, HDIM)
    priv_vals = private_values.astype(jnp.float32).reshape(requests, private_block, HEADS, HDIM)
    local_weighted = jnp.einsum("rjhgp,gphd->rjhd", pre_weights, pre_vals) + jnp.einsum(
        "rjhp,rphd->rjhd", priv_weights, priv_vals
    )
    local_peak = local_peak.reshape(all_tokens, HEADS)
    local_total = local_total.reshape(all_tokens, HEADS)
    local_weighted = local_weighted.reshape(all_tokens, model_width)
    cache_peak, cache_total, cache_weighted = merge_softmax(local_peak, local_total, local_weighted)
    key_f = fresh_keys.astype(jnp.float32).reshape(requests, NEW, HEADS, HDIM)
    new_scores = jnp.einsum("rjhd,rihd->rjhi", query_f, key_f) * score_scale
    causal = jnp.arange(NEW)[:, None] >= jnp.arange(NEW)[None, :]
    new_scores = jnp.where(causal[None, :, None, :], new_scores, BLOCKED)
    new_peak = jnp.max(new_scores, axis=3)
    new_weights = jnp.exp(new_scores - new_peak[..., None])
    new_total = jnp.sum(new_weights, axis=3).reshape(all_tokens, HEADS)
    new_weighted = jnp.einsum("rjhi,rihd->rjhd", new_weights, fresh_values).reshape(
        all_tokens, model_width
    )
    new_peak = new_peak.reshape(all_tokens, HEADS)
    final_state = merge_parts(
        (cache_peak, cache_total, cache_weighted), (new_peak, new_total, new_weighted)
    )
    attended = scale_rows(final_state[2], 1.0 / final_state[1]).astype(jnp.bfloat16)
    residual_cols = hidden + jnp.dot(attended, w_out, preferred_element_type=jnp.float32)
    full_rows = gather_cols(residual_cols)
    inv_norm = lax.rsqrt(jnp.mean(full_rows * full_rows, axis=1) + EPSILON)
    normed = (full_rows * inv_norm[:, None] * moe_gain[None, :]).astype(jnp.bfloat16)
    logits = jnp.dot(normed, router, preferred_element_type=jnp.float32)
    expert_ids = jnp.arange(logits.shape[1], dtype=jnp.int32)
    first_pick = routes[:, 0:1] == expert_ids[None, :]
    second_pick = routes[:, 1:2] == expert_ids[None, :]
    first_logit = jnp.sum(jnp.where(first_pick, logits, 0.0), axis=1)
    second_logit = jnp.sum(jnp.where(second_pick, logits, 0.0), axis=1)
    first_weight = jax.nn.sigmoid(first_logit - second_logit)
    unit_count = w_gate.shape[1]
    own_expert = own_rank * unit_count // FF
    mix_coef = first_weight * (routes[:, 0] == own_expert).astype(jnp.float32) + (
        1.0 - first_weight
    ) * (routes[:, 1] == own_expert).astype(jnp.float32)
    gate_out = jnp.dot(normed, w_gate, preferred_element_type=jnp.float32)
    up_out = jnp.dot(normed, w_up, preferred_element_type=jnp.float32)
    inner_act = (jax.nn.silu(gate_out) * up_out * mix_coef[:, None]).astype(jnp.bfloat16)
    expert_term = jnp.dot(inner_act, w_down, preferred_element_type=jnp.float32)
    return residual_cols + scatter_sum(expert_term)


def solution(mesh):
    placed = (
        P("rep", "tp"),
        P("tp"),
        P("tp", None),
        P(None, "tp"),
        P("rep", "tp", None),
        P("rep", "tp", None),
        P("rep", "tp", None),
        P("rep", "tp", None),
        P("rep"),
        P("rep"),
        P(),
        P(),
        P(None, "tp"),
        P(None, "tp"),
        P("tp", None),
        P("rep", None),
    )
    return jax.shard_map(
        on_device, mesh=mesh, in_specs=placed, out_specs=P("rep", "tp"), check_vma=False
    )
```

```python
import jax
import jax.numpy as jnp
from jax import lax
from jax.sharding import PartitionSpec as P

HEADS = 36
HDIM = 64
FF = 2880
NEW = 4


EPSILON = 1e-05
BLOCKED = -1e30


def rotate_heads(vectors, places):
    half_dim = HDIM // 2
    frequencies = 10000.0 ** (-jnp.arange(half_dim, dtype=jnp.float32) / half_dim)
    angles = places.astype(jnp.float32)[:, None] * frequencies[None, :]
    cosine = jnp.cos(angles)[:, None, :]
    sine_part = jnp.sin(angles)[:, None, :]
    first = vectors[..., :half_dim]
    second = vectors[..., half_dim:]
    return jnp.concatenate(
        [first * cosine - second * sine_part, second * cosine + first * sine_part], axis=-1
    )


def scale_rows(values, factor):
    row_count, head_count = factor.shape
    return (values.reshape(row_count, head_count, -1) * factor[..., None]).reshape(row_count, -1)


def partner_pairs(count, bit):
    return [(i, i ^ bit) for i in range(count)]


def tp_bits():
    count = lax.axis_size("tp")
    bits = []
    bit = 1
    while bit < count:
        bits.append(bit)
        bit *= 2
    return count, bits


def scatter_sum(values):
    count, bits = tp_bits()
    own_rank = lax.axis_index("tp")
    for bit in bits:
        half = values.shape[1] // 2
        side = (own_rank // bit) % 2
        keep = lax.dynamic_slice_in_dim(values, side * half, half, axis=1)
        send = lax.dynamic_slice_in_dim(values, (1 - side) * half, half, axis=1)
        values = keep + lax.ppermute(send, "tp", partner_pairs(count, bit))
    return values


def gather_cols(values):
    count, bits = tp_bits()
    own_rank = lax.axis_index("tp")
    for bit in reversed(bits):
        side = (own_rank // bit) % 2
        other = lax.ppermute(values, "tp", partner_pairs(count, bit))
        values = jnp.where(
            side == 0,
            jnp.concatenate([values, other], axis=1),
            jnp.concatenate([other, values], axis=1),
        )
    return values


def reverse_blocks(values, count):
    rows, width = values.shape
    levels = count.bit_length() - 1
    split = values.reshape((rows,) + (2,) * levels + (width // count,))
    order = (0,) + tuple(range(levels, 0, -1)) + (levels + 1,)
    return split.transpose(order).reshape(rows, width)


def merge_softmax(peak, total, weighted):
    count, bits = tp_bits()
    heads = peak.shape[1]
    for bit in reversed(bits):
        packed = jnp.concatenate([peak, total, weighted], axis=1)
        other = lax.ppermute(packed, "tp", partner_pairs(count, bit))
        other_peak = other[:, :heads]
        other_total = other[:, heads : 2 * heads]
        other_weighted = other[:, 2 * heads :]
        joint = jnp.maximum(peak, other_peak)
        own_factor = jnp.exp(peak - joint)
        other_factor = jnp.exp(other_peak - joint)
        total = total * own_factor + other_total * other_factor
        weighted = scale_rows(weighted, own_factor) + scale_rows(other_weighted, other_factor)
        peak = joint
    return peak, total, weighted


def merge_parts(first, second):
    joint_peak = jnp.maximum(first[0], second[0])
    first_factor = jnp.exp(first[0] - joint_peak)
    second_factor = jnp.exp(second[0] - joint_peak)
    totals = first[1] * first_factor + second[1] * second_factor
    weighted = scale_rows(first[2], first_factor) + scale_rows(second[2], second_factor)
    return (joint_peak, totals, weighted)


def on_device(
    hidden,
    attn_gain,
    w_qkv,
    w_out,
    prefix_keys,
    prefix_values,
    private_keys,
    private_values,
    group_ids,
    private_lengths,
    moe_gain,
    router,
    w_gate,
    w_up,
    w_down,
    routes,
):
    model_width = w_out.shape[0]
    all_tokens = hidden.shape[0]
    requests = group_ids.shape[0]
    group_count = prefix_keys.shape[0]
    prefix_block = prefix_keys.shape[1]
    private_block = private_keys.shape[1]
    own_rank = lax.axis_index("tp")
    score_scale = HDIM ** (-0.5)
    scaled = (hidden * attn_gain[None, :]).astype(jnp.bfloat16)
    partial_qkv = jnp.dot(scaled, w_qkv, preferred_element_type=jnp.float32)
    own_squares = jnp.sum(hidden * hidden, axis=1)
    qkv_width = partial_qkv.shape[1]
    tp_count = lax.axis_size("tp")
    block = qkv_width // tp_count
    packed = jnp.concatenate(
        [
            partial_qkv.reshape(all_tokens, tp_count, block),
            jnp.broadcast_to(own_squares[:, None, None], (all_tokens, tp_count, 1)),
        ],
        axis=2,
    ).reshape(all_tokens, tp_count * (block + 1))
    own_block = scatter_sum(packed)
    inv_attn = lax.rsqrt(own_block[:, block] / model_width + EPSILON)
    qkv = gather_cols((inv_attn[:, None] * own_block[:, :block]).astype(jnp.bfloat16))
    own_lengths = jnp.broadcast_to(private_lengths[:, None], (requests, NEW)).reshape(all_tokens)
    places = (
        prefix_block * lax.axis_size("tp")
        + own_lengths
        + jnp.arange(all_tokens, dtype=jnp.int32) % NEW
    )
    queries = rotate_heads(
        qkv[:, :model_width].astype(jnp.float32).reshape(all_tokens, HEADS, HDIM), places
    ).astype(jnp.bfloat16)
    fresh_keys = rotate_heads(
        qkv[:, model_width : 2 * model_width].astype(jnp.float32).reshape(all_tokens, HEADS, HDIM),
        places,
    ).astype(jnp.bfloat16)
    fresh_values = qkv[:, 2 * model_width :].astype(jnp.float32).reshape(requests, NEW, HEADS, HDIM)
    query_f = queries.astype(jnp.float32).reshape(requests, NEW, HEADS, HDIM)
    pre_keys = prefix_keys.astype(jnp.float32).reshape(group_count, prefix_block, HEADS, HDIM)
    pre_scores = jnp.einsum("rjhd,gphd->rjhgp", query_f, pre_keys) * score_scale
    member = group_ids[:, None] == jnp.arange(group_count, dtype=jnp.int32)[None, :]
    pre_scores = jnp.where(member[:, None, None, :, None], pre_scores, BLOCKED)
    priv_keys = private_keys.astype(jnp.float32).reshape(requests, private_block, HEADS, HDIM)
    priv_scores = jnp.einsum("rjhd,rphd->rjhp", query_f, priv_keys) * score_scale
    slots = own_rank * private_block + jnp.arange(private_block, dtype=jnp.int32)
    live = slots[None, :] < private_lengths[:, None]
    priv_scores = jnp.where(live[:, None, None, :], priv_scores, BLOCKED)
    local_peak = jnp.maximum(jnp.max(pre_scores, axis=(3, 4)), jnp.max(priv_scores, axis=3))
    pre_weights = jnp.exp(pre_scores - local_peak[..., None, None])
    priv_weights = jnp.exp(priv_scores - local_peak[..., None])
    local_total = jnp.sum(pre_weights, axis=(3, 4)) + jnp.sum(priv_weights, axis=3)
    pre_vals = prefix_values.astype(jnp.float32).reshape(group_count, prefix_block, HEADS, HDIM)
    priv_vals = private_values.astype(jnp.float32).reshape(requests, private_block, HEADS, HDIM)
    local_weighted = jnp.einsum("rjhgp,gphd->rjhd", pre_weights, pre_vals) + jnp.einsum(
        "rjhp,rphd->rjhd", priv_weights, priv_vals
    )
    local_peak = local_peak.reshape(all_tokens, HEADS)
    local_total = local_total.reshape(all_tokens, HEADS)
    local_weighted = local_weighted.reshape(all_tokens, model_width)
    cache_peak, cache_total, cache_weighted = merge_softmax(local_peak, local_total, local_weighted)
    key_f = fresh_keys.astype(jnp.float32).reshape(requests, NEW, HEADS, HDIM)
    new_scores = jnp.einsum("rjhd,rihd->rjhi", query_f, key_f) * score_scale
    causal = jnp.arange(NEW)[:, None] >= jnp.arange(NEW)[None, :]
    new_scores = jnp.where(causal[None, :, None, :], new_scores, BLOCKED)
    new_peak = jnp.max(new_scores, axis=3)
    new_weights = jnp.exp(new_scores - new_peak[..., None])
    new_total = jnp.sum(new_weights, axis=3).reshape(all_tokens, HEADS)
    new_weighted = jnp.einsum("rjhi,rihd->rjhd", new_weights, fresh_values).reshape(
        all_tokens, model_width
    )
    new_peak = new_peak.reshape(all_tokens, HEADS)
    final_state = merge_parts(
        (cache_peak, cache_total, cache_weighted), (new_peak, new_total, new_weighted)
    )
    attended = scale_rows(final_state[2], 1.0 / final_state[1]).astype(jnp.bfloat16)
    residual_cols = hidden + jnp.dot(attended, w_out, preferred_element_type=jnp.float32)
    full_rows = reverse_blocks(gather_cols(residual_cols), tp_count)
    inv_norm = lax.rsqrt(jnp.mean(full_rows * full_rows, axis=1) + EPSILON)
    normed = (full_rows * inv_norm[:, None] * moe_gain[None, :]).astype(jnp.bfloat16)
    logits = jnp.dot(normed, router, preferred_element_type=jnp.float32)
    expert_ids = jnp.arange(logits.shape[1], dtype=jnp.int32)
    first_pick = routes[:, 0:1] == expert_ids[None, :]
    second_pick = routes[:, 1:2] == expert_ids[None, :]
    first_logit = jnp.sum(jnp.where(first_pick, logits, 0.0), axis=1)
    second_logit = jnp.sum(jnp.where(second_pick, logits, 0.0), axis=1)
    first_weight = jax.nn.sigmoid(first_logit - second_logit)
    unit_count = w_gate.shape[1]
    own_expert = own_rank * unit_count // FF
    mix_coef = first_weight * (routes[:, 0] == own_expert).astype(jnp.float32) + (
        1.0 - first_weight
    ) * (routes[:, 1] == own_expert).astype(jnp.float32)
    gate_out = jnp.dot(normed, w_gate, preferred_element_type=jnp.float32)
    up_out = jnp.dot(normed, w_up, preferred_element_type=jnp.float32)
    inner_act = (jax.nn.silu(gate_out) * up_out * mix_coef[:, None]).astype(jnp.bfloat16)
    expert_term = jnp.dot(inner_act, w_down, preferred_element_type=jnp.float32)
    return residual_cols + scatter_sum(reverse_blocks(expert_term, tp_count))


def solution(mesh):
    placed = (
        P("rep", "tp"),
        P("tp"),
        P("tp", None),
        P(None, "tp"),
        P("rep", "tp", None),
        P("rep", "tp", None),
        P("rep", "tp", None),
        P("rep", "tp", None),
        P("rep"),
        P("rep"),
        P(),
        P(),
        P(None, "tp"),
        P(None, "tp"),
        P("tp", None),
        P("rep", None),
    )
    return jax.shard_map(
        on_device, mesh=mesh, in_specs=placed, out_specs=P("rep", "tp"), check_vma=False
    )
```

```python
import jax
import jax.numpy as jnp
from jax import lax
from jax.sharding import PartitionSpec as P

HEADS = 36
HDIM = 64
FF = 2880
NEW = 4


EPSILON = 1e-05
BLOCKED = -1e30


def rotate_heads(vectors, places):
    half_dim = HDIM // 2
    frequencies = 10000.0 ** (-jnp.arange(half_dim, dtype=jnp.float32) / half_dim)
    angles = places.astype(jnp.float32)[:, None] * frequencies[None, :]
    cosine = jnp.cos(angles)[:, None, :]
    sine_part = jnp.sin(angles)[:, None, :]
    first = vectors[..., :half_dim]
    second = vectors[..., half_dim:]
    return jnp.concatenate(
        [first * cosine - second * sine_part, second * cosine + first * sine_part], axis=-1
    )


def scale_rows(values, factor):
    row_count, head_count = factor.shape
    return (values.reshape(row_count, head_count, -1) * factor[..., None]).reshape(row_count, -1)


def partner_pairs(count, bit):
    return [(i, i ^ bit) for i in range(count)]


def tp_bits():
    count = lax.axis_size("tp")
    bits = []
    bit = 1
    while bit < count:
        bits.append(bit)
        bit *= 2
    return count, bits


def scatter_sum(values):
    count, bits = tp_bits()
    own_rank = lax.axis_index("tp")
    for bit in bits:
        half = values.shape[1] // 2
        side = (own_rank // bit) % 2
        keep = lax.dynamic_slice_in_dim(values, side * half, half, axis=1)
        send = lax.dynamic_slice_in_dim(values, (1 - side) * half, half, axis=1)
        values = keep + lax.ppermute(send, "tp", partner_pairs(count, bit))
    return values


def gather_cols(values, axis=1):
    count, bits = tp_bits()
    own_rank = lax.axis_index("tp")
    for bit in reversed(bits):
        side = (own_rank // bit) % 2
        other = lax.ppermute(values, "tp", partner_pairs(count, bit))
        values = jnp.where(
            side == 0,
            jnp.concatenate([values, other], axis=axis),
            jnp.concatenate([other, values], axis=axis),
        )
    return values


def reversed_rank(count):
    own_rank = lax.axis_index("tp")
    levels = count.bit_length() - 1
    position = 0
    for level in range(levels):
        position = position + ((own_rank // 2**level) % 2) * 2 ** (levels - 1 - level)
    return position


def merge_rows(first, second):
    joint = jnp.maximum(first[:, -1:], second[:, -1:])
    first_factor = jnp.exp(first[:, -1:] - joint)
    second_factor = jnp.exp(second[:, -1:] - joint)
    body = first[:, :-1] * first_factor + second[:, :-1] * second_factor
    return jnp.concatenate([body, joint], axis=1)


def scatter_merge(rows):
    count, bits = tp_bits()
    own_rank = lax.axis_index("tp")
    for bit in bits:
        half = rows.shape[0] // 2
        side = (own_rank // bit) % 2
        keep = lax.dynamic_slice_in_dim(rows, side * half, half, axis=0)
        send = lax.dynamic_slice_in_dim(rows, (1 - side) * half, half, axis=0)
        rows = merge_rows(keep, lax.ppermute(send, "tp", partner_pairs(count, bit)))
    return rows


def state_rows(peak, total, weighted):
    row_count = peak.shape[0] * peak.shape[1]
    return jnp.concatenate(
        [weighted.reshape(row_count, -1), total.reshape(row_count, 1), peak.reshape(row_count, 1)],
        axis=1,
    )


def reverse_blocks(values, count):
    rows, width = values.shape
    levels = count.bit_length() - 1
    split = values.reshape((rows,) + (2,) * levels + (width // count,))
    order = (0,) + tuple(range(levels, 0, -1)) + (levels + 1,)
    return split.transpose(order).reshape(rows, width)


def on_device(
    hidden,
    attn_gain,
    w_qkv,
    w_out,
    prefix_keys,
    prefix_values,
    private_keys,
    private_values,
    group_ids,
    private_lengths,
    moe_gain,
    router,
    w_gate,
    w_up,
    w_down,
    routes,
):
    model_width = w_out.shape[0]
    all_tokens = hidden.shape[0]
    requests = group_ids.shape[0]
    group_count = prefix_keys.shape[0]
    prefix_block = prefix_keys.shape[1]
    private_block = private_keys.shape[1]
    own_rank = lax.axis_index("tp")
    score_scale = HDIM ** (-0.5)
    scaled = (hidden * attn_gain[None, :]).astype(jnp.bfloat16)
    partial_qkv = jnp.dot(scaled, w_qkv, preferred_element_type=jnp.float32)
    own_squares = jnp.sum(hidden * hidden, axis=1)
    qkv_width = partial_qkv.shape[1]
    tp_count = lax.axis_size("tp")
    block = qkv_width // tp_count
    packed = jnp.concatenate(
        [
            partial_qkv.reshape(all_tokens, tp_count, block),
            jnp.broadcast_to(own_squares[:, None, None], (all_tokens, tp_count, 1)),
        ],
        axis=2,
    ).reshape(all_tokens, tp_count * (block + 1))
    own_block = scatter_sum(packed)
    inv_attn = lax.rsqrt(own_block[:, block] / model_width + EPSILON)
    qkv = gather_cols((inv_attn[:, None] * own_block[:, :block]).astype(jnp.bfloat16))
    own_lengths = jnp.broadcast_to(private_lengths[:, None], (requests, NEW)).reshape(all_tokens)
    places = (
        prefix_block * lax.axis_size("tp")
        + own_lengths
        + jnp.arange(all_tokens, dtype=jnp.int32) % NEW
    )
    queries = rotate_heads(
        qkv[:, :model_width].astype(jnp.float32).reshape(all_tokens, HEADS, HDIM), places
    ).astype(jnp.bfloat16)
    fresh_keys = rotate_heads(
        qkv[:, model_width : 2 * model_width].astype(jnp.float32).reshape(all_tokens, HEADS, HDIM),
        places,
    ).astype(jnp.bfloat16)
    fresh_values = qkv[:, 2 * model_width :].astype(jnp.float32).reshape(requests, NEW, HEADS, HDIM)
    query_f = queries.astype(jnp.float32).reshape(requests, NEW, HEADS, HDIM)
    pre_keys = prefix_keys.astype(jnp.float32).reshape(group_count, prefix_block, HEADS, HDIM)
    pre_scores = jnp.einsum("rjhd,gphd->rjhgp", query_f, pre_keys) * score_scale
    member = group_ids[:, None] == jnp.arange(group_count, dtype=jnp.int32)[None, :]
    pre_scores = jnp.where(member[:, None, None, :, None], pre_scores, BLOCKED)
    priv_keys = private_keys.astype(jnp.float32).reshape(requests, private_block, HEADS, HDIM)
    priv_scores = jnp.einsum("rjhd,rphd->rjhp", query_f, priv_keys) * score_scale
    slots = own_rank * private_block + jnp.arange(private_block, dtype=jnp.int32)
    live = slots[None, :] < private_lengths[:, None]
    priv_scores = jnp.where(live[:, None, None, :], priv_scores, BLOCKED)
    local_peak = jnp.maximum(jnp.max(pre_scores, axis=(3, 4)), jnp.max(priv_scores, axis=3))
    pre_weights = jnp.exp(pre_scores - local_peak[..., None, None])
    priv_weights = jnp.exp(priv_scores - local_peak[..., None])
    local_total = jnp.sum(pre_weights, axis=(3, 4)) + jnp.sum(priv_weights, axis=3)
    pre_vals = prefix_values.astype(jnp.float32).reshape(group_count, prefix_block, HEADS, HDIM)
    priv_vals = private_values.astype(jnp.float32).reshape(requests, private_block, HEADS, HDIM)
    local_weighted = jnp.einsum("rjhgp,gphd->rjhd", pre_weights, pre_vals) + jnp.einsum(
        "rjhp,rphd->rjhd", priv_weights, priv_vals
    )
    local_peak = local_peak.reshape(all_tokens, HEADS)
    local_total = local_total.reshape(all_tokens, HEADS)
    local_weighted = local_weighted.reshape(all_tokens, model_width)
    cache_rows = scatter_merge(state_rows(local_peak, local_total, local_weighted))
    key_f = fresh_keys.astype(jnp.float32).reshape(requests, NEW, HEADS, HDIM)
    new_scores = jnp.einsum("rjhd,rihd->rjhi", query_f, key_f) * score_scale
    causal = jnp.arange(NEW)[:, None] >= jnp.arange(NEW)[None, :]
    new_scores = jnp.where(causal[None, :, None, :], new_scores, BLOCKED)
    new_peak = jnp.max(new_scores, axis=3)
    new_weights = jnp.exp(new_scores - new_peak[..., None])
    new_total = jnp.sum(new_weights, axis=3).reshape(all_tokens, HEADS)
    new_weighted = jnp.einsum("rjhi,rihd->rjhd", new_weights, fresh_values).reshape(
        all_tokens, model_width
    )
    new_peak = new_peak.reshape(all_tokens, HEADS)
    new_rows = state_rows(new_peak, new_total, new_weighted)
    own_count = cache_rows.shape[0]
    new_rows = lax.dynamic_slice_in_dim(new_rows, reversed_rank(tp_count) * own_count, own_count, axis=0)
    final_rows = merge_rows(cache_rows, new_rows)
    attended_rows = (final_rows[:, :HDIM] / final_rows[:, HDIM : HDIM + 1]).astype(jnp.bfloat16)
    attended = gather_cols(attended_rows, axis=0).reshape(all_tokens, model_width)
    residual_cols = hidden + jnp.dot(attended, w_out, preferred_element_type=jnp.float32)
    full_rows = reverse_blocks(gather_cols(residual_cols), tp_count)
    inv_norm = lax.rsqrt(jnp.mean(full_rows * full_rows, axis=1) + EPSILON)
    normed = (full_rows * inv_norm[:, None] * moe_gain[None, :]).astype(jnp.bfloat16)
    logits = jnp.dot(normed, router, preferred_element_type=jnp.float32)
    expert_ids = jnp.arange(logits.shape[1], dtype=jnp.int32)
    first_pick = routes[:, 0:1] == expert_ids[None, :]
    second_pick = routes[:, 1:2] == expert_ids[None, :]
    first_logit = jnp.sum(jnp.where(first_pick, logits, 0.0), axis=1)
    second_logit = jnp.sum(jnp.where(second_pick, logits, 0.0), axis=1)
    first_weight = jax.nn.sigmoid(first_logit - second_logit)
    unit_count = w_gate.shape[1]
    own_expert = own_rank * unit_count // FF
    mix_coef = first_weight * (routes[:, 0] == own_expert).astype(jnp.float32) + (
        1.0 - first_weight
    ) * (routes[:, 1] == own_expert).astype(jnp.float32)
    gate_out = jnp.dot(normed, w_gate, preferred_element_type=jnp.float32)
    up_out = jnp.dot(normed, w_up, preferred_element_type=jnp.float32)
    inner_act = (jax.nn.silu(gate_out) * up_out * mix_coef[:, None]).astype(jnp.bfloat16)
    expert_term = jnp.dot(inner_act, w_down, preferred_element_type=jnp.float32)
    return residual_cols + scatter_sum(reverse_blocks(expert_term, tp_count))


def solution(mesh):
    placed = (
        P("rep", "tp"),
        P("tp"),
        P("tp", None),
        P(None, "tp"),
        P("rep", "tp", None),
        P("rep", "tp", None),
        P("rep", "tp", None),
        P("rep", "tp", None),
        P("rep"),
        P("rep"),
        P(),
        P(),
        P(None, "tp"),
        P(None, "tp"),
        P("tp", None),
        P("rep", None),
    )
    return jax.shard_map(
        on_device, mesh=mesh, in_specs=placed, out_specs=P("rep", "tp"), check_vma=False
    )
```

```python
import jax
import jax.numpy as jnp
from jax import lax
from jax.sharding import PartitionSpec as P

HEADS = 36
HDIM = 64
FF = 2880
NEW = 4


EPSILON = 1e-05
BLOCKED = -1e30


def rotate_heads(vectors, places):
    half_dim = HDIM // 2
    frequencies = 10000.0 ** (-jnp.arange(half_dim, dtype=jnp.float32) / half_dim)
    angles = places.astype(jnp.float32)[:, None] * frequencies[None, :]
    cosine = jnp.cos(angles)[:, None, :]
    sine_part = jnp.sin(angles)[:, None, :]
    first = vectors[..., :half_dim]
    second = vectors[..., half_dim:]
    return jnp.concatenate(
        [first * cosine - second * sine_part, second * cosine + first * sine_part], axis=-1
    )


def scale_rows(values, factor):
    row_count, head_count = factor.shape
    return (values.reshape(row_count, head_count, -1) * factor[..., None]).reshape(row_count, -1)


def partner_pairs(count, bit):
    return [(i, i ^ bit) for i in range(count)]


def tp_bits():
    count = lax.axis_size("tp")
    bits = []
    bit = 1
    while bit < count:
        bits.append(bit)
        bit *= 2
    return count, bits


def scatter_sum(values, bits=None):
    count, all_bits = tp_bits()
    bits = all_bits if bits is None else bits
    own_rank = lax.axis_index("tp")
    for bit in bits:
        half = values.shape[1] // 2
        side = (own_rank // bit) % 2
        keep = lax.dynamic_slice_in_dim(values, side * half, half, axis=1)
        send = lax.dynamic_slice_in_dim(values, (1 - side) * half, half, axis=1)
        values = keep + lax.ppermute(send, "tp", partner_pairs(count, bit))
    return values


def gather_cols(values, axis=1, bits=None):
    count, all_bits = tp_bits()
    bits = all_bits if bits is None else bits
    own_rank = lax.axis_index("tp")
    for bit in reversed(bits):
        side = (own_rank // bit) % 2
        other = lax.ppermute(values, "tp", partner_pairs(count, bit))
        values = jnp.where(
            side == 0,
            jnp.concatenate([values, other], axis=axis),
            jnp.concatenate([other, values], axis=axis),
        )
    return values


def kept_position(bits):
    own_rank = lax.axis_index("tp")
    position = 0
    for level, bit in enumerate(bits):
        position = position + ((own_rank // bit) % 2) * 2 ** (len(bits) - 1 - level)
    return position


def exchange_sum(values, bits):
    count, _ = tp_bits()
    for bit in bits:
        values = values + lax.ppermute(values, "tp", partner_pairs(count, bit))
    return values


def exchange_merge(rows, bits):
    count, _ = tp_bits()
    for bit in bits:
        rows = merge_rows(rows, lax.ppermute(rows, "tp", partner_pairs(count, bit)))
    return rows


def merge_rows(first, second):
    joint = jnp.maximum(first[:, -1:], second[:, -1:])
    first_factor = jnp.exp(first[:, -1:] - joint)
    second_factor = jnp.exp(second[:, -1:] - joint)
    body = first[:, :-1] * first_factor + second[:, :-1] * second_factor
    return jnp.concatenate([body, joint], axis=1)


def scatter_merge(rows, bits):
    count, _ = tp_bits()
    own_rank = lax.axis_index("tp")
    for bit in bits:
        half = rows.shape[0] // 2
        side = (own_rank // bit) % 2
        keep = lax.dynamic_slice_in_dim(rows, side * half, half, axis=0)
        send = lax.dynamic_slice_in_dim(rows, (1 - side) * half, half, axis=0)
        rows = merge_rows(keep, lax.ppermute(send, "tp", partner_pairs(count, bit)))
    return rows


def state_rows(peak, total, weighted):
    row_count = peak.shape[0] * peak.shape[1]
    return jnp.concatenate(
        [weighted.reshape(row_count, -1), total.reshape(row_count, 1), peak.reshape(row_count, 1)],
        axis=1,
    )


def reverse_blocks(values, count):
    rows, width = values.shape
    levels = count.bit_length() - 1
    split = values.reshape((rows,) + (2,) * levels + (width // count,))
    order = (0,) + tuple(range(levels, 0, -1)) + (levels + 1,)
    return split.transpose(order).reshape(rows, width)


def on_device(
    hidden,
    attn_gain,
    w_qkv,
    w_out,
    prefix_keys,
    prefix_values,
    private_keys,
    private_values,
    group_ids,
    private_lengths,
    moe_gain,
    router,
    w_gate,
    w_up,
    w_down,
    routes,
):
    model_width = w_out.shape[0]
    all_tokens = hidden.shape[0]
    requests = group_ids.shape[0]
    group_count = prefix_keys.shape[0]
    prefix_block = prefix_keys.shape[1]
    private_block = private_keys.shape[1]
    own_rank = lax.axis_index("tp")
    score_scale = HDIM ** (-0.5)
    scaled = (hidden * attn_gain[None, :]).astype(jnp.bfloat16)
    partial_qkv = jnp.dot(scaled, w_qkv, preferred_element_type=jnp.float32)
    own_squares = jnp.sum(hidden * hidden, axis=1)
    qkv_width = partial_qkv.shape[1]
    tp_count = lax.axis_size("tp")
    block = qkv_width // tp_count
    packed = jnp.concatenate(
        [
            partial_qkv.reshape(all_tokens, tp_count, block),
            jnp.broadcast_to(own_squares[:, None, None], (all_tokens, tp_count, 1)),
        ],
        axis=2,
    ).reshape(all_tokens, tp_count * (block + 1))
    _, all_bits = tp_bits()
    near_bits = all_bits[: len(all_bits) // 2]
    far_bits = all_bits[len(all_bits) // 2 :]
    own_block = exchange_sum(scatter_sum(packed, near_bits), far_bits)
    own_block = own_block.reshape(all_tokens, -1, block + 1)
    inv_attn = lax.rsqrt(own_block[:, 0, block] / model_width + EPSILON)
    own_qkv = (inv_attn[:, None, None] * own_block[:, :, :block]).astype(jnp.bfloat16)
    qkv = gather_cols(own_qkv.reshape(all_tokens, -1), bits=near_bits)
    own_lengths = jnp.broadcast_to(private_lengths[:, None], (requests, NEW)).reshape(all_tokens)
    places = (
        prefix_block * lax.axis_size("tp")
        + own_lengths
        + jnp.arange(all_tokens, dtype=jnp.int32) % NEW
    )
    queries = rotate_heads(
        qkv[:, :model_width].astype(jnp.float32).reshape(all_tokens, HEADS, HDIM), places
    ).astype(jnp.bfloat16)
    fresh_keys = rotate_heads(
        qkv[:, model_width : 2 * model_width].astype(jnp.float32).reshape(all_tokens, HEADS, HDIM),
        places,
    ).astype(jnp.bfloat16)
    fresh_values = qkv[:, 2 * model_width :].astype(jnp.float32).reshape(requests, NEW, HEADS, HDIM)
    query_f = queries.astype(jnp.float32).reshape(requests, NEW, HEADS, HDIM)
    pre_keys = prefix_keys.astype(jnp.float32).reshape(group_count, prefix_block, HEADS, HDIM)
    pre_scores = jnp.einsum("rjhd,gphd->rjhgp", query_f, pre_keys) * score_scale
    member = group_ids[:, None] == jnp.arange(group_count, dtype=jnp.int32)[None, :]
    pre_scores = jnp.where(member[:, None, None, :, None], pre_scores, BLOCKED)
    priv_keys = private_keys.astype(jnp.float32).reshape(requests, private_block, HEADS, HDIM)
    priv_scores = jnp.einsum("rjhd,rphd->rjhp", query_f, priv_keys) * score_scale
    slots = own_rank * private_block + jnp.arange(private_block, dtype=jnp.int32)
    live = slots[None, :] < private_lengths[:, None]
    priv_scores = jnp.where(live[:, None, None, :], priv_scores, BLOCKED)
    local_peak = jnp.maximum(jnp.max(pre_scores, axis=(3, 4)), jnp.max(priv_scores, axis=3))
    pre_weights = jnp.exp(pre_scores - local_peak[..., None, None])
    priv_weights = jnp.exp(priv_scores - local_peak[..., None])
    local_total = jnp.sum(pre_weights, axis=(3, 4)) + jnp.sum(priv_weights, axis=3)
    pre_vals = prefix_values.astype(jnp.float32).reshape(group_count, prefix_block, HEADS, HDIM)
    priv_vals = private_values.astype(jnp.float32).reshape(requests, private_block, HEADS, HDIM)
    local_weighted = jnp.einsum("rjhgp,gphd->rjhd", pre_weights, pre_vals) + jnp.einsum(
        "rjhp,rphd->rjhd", priv_weights, priv_vals
    )
    local_peak = local_peak.reshape(all_tokens, HEADS)
    local_total = local_total.reshape(all_tokens, HEADS)
    local_weighted = local_weighted.reshape(all_tokens, model_width)
    cache_rows = scatter_merge(state_rows(local_peak, local_total, local_weighted), near_bits)
    cache_rows = exchange_merge(cache_rows, far_bits)
    key_f = fresh_keys.astype(jnp.float32).reshape(requests, NEW, HEADS, HDIM)
    new_scores = jnp.einsum("rjhd,rihd->rjhi", query_f, key_f) * score_scale
    causal = jnp.arange(NEW)[:, None] >= jnp.arange(NEW)[None, :]
    new_scores = jnp.where(causal[None, :, None, :], new_scores, BLOCKED)
    new_peak = jnp.max(new_scores, axis=3)
    new_weights = jnp.exp(new_scores - new_peak[..., None])
    new_total = jnp.sum(new_weights, axis=3).reshape(all_tokens, HEADS)
    new_weighted = jnp.einsum("rjhi,rihd->rjhd", new_weights, fresh_values).reshape(
        all_tokens, model_width
    )
    new_peak = new_peak.reshape(all_tokens, HEADS)
    new_rows = state_rows(new_peak, new_total, new_weighted)
    own_count = cache_rows.shape[0]
    new_rows = lax.dynamic_slice_in_dim(new_rows, kept_position(near_bits) * own_count, own_count, axis=0)
    final_rows = merge_rows(cache_rows, new_rows)
    attended_rows = (final_rows[:, :HDIM] / final_rows[:, HDIM : HDIM + 1]).astype(jnp.bfloat16)
    attended = gather_cols(attended_rows, axis=0, bits=near_bits).reshape(all_tokens, model_width)
    residual_cols = hidden + jnp.dot(attended, w_out, preferred_element_type=jnp.float32)
    full_rows = reverse_blocks(gather_cols(residual_cols), tp_count)
    inv_norm = lax.rsqrt(jnp.mean(full_rows * full_rows, axis=1) + EPSILON)
    normed = (full_rows * inv_norm[:, None] * moe_gain[None, :]).astype(jnp.bfloat16)
    logits = jnp.dot(normed, router, preferred_element_type=jnp.float32)
    expert_ids = jnp.arange(logits.shape[1], dtype=jnp.int32)
    first_pick = routes[:, 0:1] == expert_ids[None, :]
    second_pick = routes[:, 1:2] == expert_ids[None, :]
    first_logit = jnp.sum(jnp.where(first_pick, logits, 0.0), axis=1)
    second_logit = jnp.sum(jnp.where(second_pick, logits, 0.0), axis=1)
    first_weight = jax.nn.sigmoid(first_logit - second_logit)
    unit_count = w_gate.shape[1]
    own_expert = own_rank * unit_count // FF
    mix_coef = first_weight * (routes[:, 0] == own_expert).astype(jnp.float32) + (
        1.0 - first_weight
    ) * (routes[:, 1] == own_expert).astype(jnp.float32)
    gate_out = jnp.dot(normed, w_gate, preferred_element_type=jnp.float32)
    up_out = jnp.dot(normed, w_up, preferred_element_type=jnp.float32)
    inner_act = (jax.nn.silu(gate_out) * up_out * mix_coef[:, None]).astype(jnp.bfloat16)
    expert_term = jnp.dot(inner_act, w_down, preferred_element_type=jnp.float32)
    return residual_cols + scatter_sum(reverse_blocks(expert_term, tp_count))


def solution(mesh):
    placed = (
        P("rep", "tp"),
        P("tp"),
        P("tp", None),
        P(None, "tp"),
        P("rep", "tp", None),
        P("rep", "tp", None),
        P("rep", "tp", None),
        P("rep", "tp", None),
        P("rep"),
        P("rep"),
        P(),
        P(),
        P(None, "tp"),
        P(None, "tp"),
        P("tp", None),
        P("rep", None),
    )
    return jax.shard_map(
        on_device, mesh=mesh, in_specs=placed, out_specs=P("rep", "tp"), check_vma=False
    )
```

```python
import jax
import jax.numpy as jnp
from jax import lax
from jax.sharding import PartitionSpec as P

HEADS = 36
HDIM = 64
FF = 2880
NEW = 4


EPSILON = 1e-05
BLOCKED = -1e30


def rotate_heads(vectors, places):
    half_dim = HDIM // 2
    frequencies = 10000.0 ** (-jnp.arange(half_dim, dtype=jnp.float32) / half_dim)
    angles = places.astype(jnp.float32)[:, None] * frequencies[None, :]
    cosine = jnp.cos(angles)[:, None, :]
    sine_part = jnp.sin(angles)[:, None, :]
    first = vectors[..., :half_dim]
    second = vectors[..., half_dim:]
    return jnp.concatenate(
        [first * cosine - second * sine_part, second * cosine + first * sine_part], axis=-1
    )


def scale_rows(values, factor):
    row_count, head_count = factor.shape
    return (values.reshape(row_count, head_count, -1) * factor[..., None]).reshape(row_count, -1)


def partner_pairs(count, bit):
    return [(i, i ^ bit) for i in range(count)]


def tp_bits():
    count = lax.axis_size("tp")
    bits = []
    bit = 1
    while bit < count:
        bits.append(bit)
        bit *= 2
    return count, bits


def scatter_sum(values, bits=None):
    count, all_bits = tp_bits()
    bits = all_bits if bits is None else bits
    own_rank = lax.axis_index("tp")
    for bit in bits:
        half = values.shape[1] // 2
        side = (own_rank // bit) % 2
        keep = lax.dynamic_slice_in_dim(values, side * half, half, axis=1)
        send = lax.dynamic_slice_in_dim(values, (1 - side) * half, half, axis=1)
        values = keep + lax.ppermute(send, "tp", partner_pairs(count, bit))
    return values


def gather_cols(values, axis=1, bits=None):
    count, all_bits = tp_bits()
    bits = all_bits if bits is None else bits
    own_rank = lax.axis_index("tp")
    for bit in reversed(bits):
        side = (own_rank // bit) % 2
        other = lax.ppermute(values, "tp", partner_pairs(count, bit))
        values = jnp.where(
            side == 0,
            jnp.concatenate([values, other], axis=axis),
            jnp.concatenate([other, values], axis=axis),
        )
    return values


def kept_position(bits):
    own_rank = lax.axis_index("tp")
    position = 0
    for level, bit in enumerate(bits):
        position = position + ((own_rank // bit) % 2) * 2 ** (len(bits) - 1 - level)
    return position


def exchange_sum(values, bits):
    count, _ = tp_bits()
    for bit in bits:
        values = values + lax.ppermute(values, "tp", partner_pairs(count, bit))
    return values


def exchange_merge(rows, bits):
    count, _ = tp_bits()
    for bit in bits:
        rows = merge_rows(rows, lax.ppermute(rows, "tp", partner_pairs(count, bit)))
    return rows


def merge_rows(first, second):
    joint = jnp.maximum(first[:, -1:], second[:, -1:])
    first_factor = jnp.exp(first[:, -1:] - joint)
    second_factor = jnp.exp(second[:, -1:] - joint)
    body = first[:, :-1] * first_factor + second[:, :-1] * second_factor
    return jnp.concatenate([body, joint], axis=1)


def scatter_merge(rows, bits):
    count, _ = tp_bits()
    own_rank = lax.axis_index("tp")
    for bit in bits:
        half = rows.shape[0] // 2
        side = (own_rank // bit) % 2
        keep = lax.dynamic_slice_in_dim(rows, side * half, half, axis=0)
        send = lax.dynamic_slice_in_dim(rows, (1 - side) * half, half, axis=0)
        rows = merge_rows(keep, lax.ppermute(send, "tp", partner_pairs(count, bit)))
    return rows


def state_rows(peak, total, weighted):
    row_count = peak.shape[0] * peak.shape[1]
    return jnp.concatenate(
        [weighted.reshape(row_count, -1), total.reshape(row_count, 1), peak.reshape(row_count, 1)],
        axis=1,
    )


def reverse_blocks(values, count):
    rows, width = values.shape
    levels = count.bit_length() - 1
    split = values.reshape((rows,) + (2,) * levels + (width // count,))
    order = (0,) + tuple(range(levels, 0, -1)) + (levels + 1,)
    return split.transpose(order).reshape(rows, width)


def on_device(
    hidden,
    attn_gain,
    w_qkv,
    w_out,
    prefix_keys,
    prefix_values,
    private_keys,
    private_values,
    group_ids,
    private_lengths,
    moe_gain,
    router,
    w_gate,
    w_up,
    w_down,
    routes,
):
    model_width = w_out.shape[0]
    all_tokens = hidden.shape[0]
    requests = group_ids.shape[0]
    group_count = prefix_keys.shape[0]
    prefix_block = prefix_keys.shape[1]
    private_block = private_keys.shape[1]
    own_rank = lax.axis_index("tp")
    score_scale = HDIM ** (-0.5)
    scaled = (hidden * attn_gain[None, :]).astype(jnp.bfloat16)
    partial_qkv = jnp.dot(scaled, w_qkv, preferred_element_type=jnp.float32)
    own_squares = jnp.sum(hidden * hidden, axis=1)
    tp_count = lax.axis_size("tp")
    _, all_bits = tp_bits()
    near_bits = all_bits[: len(all_bits) // 2]
    far_bits = all_bits[len(all_bits) // 2 :]
    query_block = model_width // tp_count
    packed = jnp.concatenate(
        [
            partial_qkv[:, :model_width].reshape(all_tokens, tp_count, query_block),
            jnp.broadcast_to(own_squares[:, None, None], (all_tokens, tp_count, 1)),
        ],
        axis=2,
    ).reshape(all_tokens, tp_count * (query_block + 1))
    own_block = exchange_sum(scatter_sum(packed, near_bits), far_bits)
    own_block = own_block.reshape(all_tokens, -1, query_block + 1)
    inv_attn = lax.rsqrt(own_block[:, 0, query_block] / model_width + EPSILON)
    own_query = (inv_attn[:, None, None] * own_block[:, :, :query_block]).astype(jnp.bfloat16)
    query_cols = gather_cols(own_query.reshape(all_tokens, -1), bits=near_bits)
    own_kv = exchange_sum(scatter_sum(partial_qkv[:, model_width:], near_bits), far_bits)
    own_kv = (inv_attn[:, None] * own_kv).astype(jnp.bfloat16)
    kv_cols = gather_cols(own_kv, bits=near_bits)
    qkv = jnp.concatenate([query_cols, kv_cols], axis=1)
    own_lengths = jnp.broadcast_to(private_lengths[:, None], (requests, NEW)).reshape(all_tokens)
    places = (
        prefix_block * lax.axis_size("tp")
        + own_lengths
        + jnp.arange(all_tokens, dtype=jnp.int32) % NEW
    )
    queries = rotate_heads(
        qkv[:, :model_width].astype(jnp.float32).reshape(all_tokens, HEADS, HDIM), places
    ).astype(jnp.bfloat16)
    fresh_keys = rotate_heads(
        qkv[:, model_width : 2 * model_width].astype(jnp.float32).reshape(all_tokens, HEADS, HDIM),
        places,
    ).astype(jnp.bfloat16)
    fresh_values = qkv[:, 2 * model_width :].astype(jnp.float32).reshape(requests, NEW, HEADS, HDIM)
    query_f = queries.astype(jnp.float32).reshape(requests, NEW, HEADS, HDIM)
    pre_keys = prefix_keys.astype(jnp.float32).reshape(group_count, prefix_block, HEADS, HDIM)
    pre_scores = jnp.einsum("rjhd,gphd->rjhgp", query_f, pre_keys) * score_scale
    member = group_ids[:, None] == jnp.arange(group_count, dtype=jnp.int32)[None, :]
    pre_scores = jnp.where(member[:, None, None, :, None], pre_scores, BLOCKED)
    priv_keys = private_keys.astype(jnp.float32).reshape(requests, private_block, HEADS, HDIM)
    priv_scores = jnp.einsum("rjhd,rphd->rjhp", query_f, priv_keys) * score_scale
    slots = own_rank * private_block + jnp.arange(private_block, dtype=jnp.int32)
    live = slots[None, :] < private_lengths[:, None]
    priv_scores = jnp.where(live[:, None, None, :], priv_scores, BLOCKED)
    local_peak = jnp.maximum(jnp.max(pre_scores, axis=(3, 4)), jnp.max(priv_scores, axis=3))
    pre_weights = jnp.exp(pre_scores - local_peak[..., None, None])
    priv_weights = jnp.exp(priv_scores - local_peak[..., None])
    local_total = jnp.sum(pre_weights, axis=(3, 4)) + jnp.sum(priv_weights, axis=3)
    pre_vals = prefix_values.astype(jnp.float32).reshape(group_count, prefix_block, HEADS, HDIM)
    priv_vals = private_values.astype(jnp.float32).reshape(requests, private_block, HEADS, HDIM)
    local_weighted = jnp.einsum("rjhgp,gphd->rjhd", pre_weights, pre_vals) + jnp.einsum(
        "rjhp,rphd->rjhd", priv_weights, priv_vals
    )
    local_peak = local_peak.reshape(all_tokens, HEADS)
    local_total = local_total.reshape(all_tokens, HEADS)
    local_weighted = local_weighted.reshape(all_tokens, model_width)
    cache_rows = scatter_merge(state_rows(local_peak, local_total, local_weighted), near_bits)
    cache_rows = exchange_merge(cache_rows, far_bits)
    key_f = fresh_keys.astype(jnp.float32).reshape(requests, NEW, HEADS, HDIM)
    new_scores = jnp.einsum("rjhd,rihd->rjhi", query_f, key_f) * score_scale
    causal = jnp.arange(NEW)[:, None] >= jnp.arange(NEW)[None, :]
    new_scores = jnp.where(causal[None, :, None, :], new_scores, BLOCKED)
    new_peak = jnp.max(new_scores, axis=3)
    new_weights = jnp.exp(new_scores - new_peak[..., None])
    new_total = jnp.sum(new_weights, axis=3).reshape(all_tokens, HEADS)
    new_weighted = jnp.einsum("rjhi,rihd->rjhd", new_weights, fresh_values).reshape(
        all_tokens, model_width
    )
    new_peak = new_peak.reshape(all_tokens, HEADS)
    new_rows = state_rows(new_peak, new_total, new_weighted)
    own_count = cache_rows.shape[0]
    new_rows = lax.dynamic_slice_in_dim(new_rows, kept_position(near_bits) * own_count, own_count, axis=0)
    final_rows = merge_rows(cache_rows, new_rows)
    attended_rows = (final_rows[:, :HDIM] / final_rows[:, HDIM : HDIM + 1]).astype(jnp.bfloat16)
    attended = gather_cols(attended_rows, axis=0, bits=near_bits).reshape(all_tokens, model_width)
    residual_cols = hidden + jnp.dot(attended, w_out, preferred_element_type=jnp.float32)
    full_rows = reverse_blocks(gather_cols(residual_cols), tp_count)
    inv_norm = lax.rsqrt(jnp.mean(full_rows * full_rows, axis=1) + EPSILON)
    normed = (full_rows * inv_norm[:, None] * moe_gain[None, :]).astype(jnp.bfloat16)
    logits = jnp.dot(normed, router, preferred_element_type=jnp.float32)
    expert_ids = jnp.arange(logits.shape[1], dtype=jnp.int32)
    first_pick = routes[:, 0:1] == expert_ids[None, :]
    second_pick = routes[:, 1:2] == expert_ids[None, :]
    first_logit = jnp.sum(jnp.where(first_pick, logits, 0.0), axis=1)
    second_logit = jnp.sum(jnp.where(second_pick, logits, 0.0), axis=1)
    first_weight = jax.nn.sigmoid(first_logit - second_logit)
    unit_count = w_gate.shape[1]
    own_expert = own_rank * unit_count // FF
    mix_coef = first_weight * (routes[:, 0] == own_expert).astype(jnp.float32) + (
        1.0 - first_weight
    ) * (routes[:, 1] == own_expert).astype(jnp.float32)
    gate_out = jnp.dot(normed, w_gate, preferred_element_type=jnp.float32)
    up_out = jnp.dot(normed, w_up, preferred_element_type=jnp.float32)
    inner_act = (jax.nn.silu(gate_out) * up_out * mix_coef[:, None]).astype(jnp.bfloat16)
    expert_term = jnp.dot(inner_act, w_down, preferred_element_type=jnp.float32)
    return residual_cols + scatter_sum(reverse_blocks(expert_term, tp_count))


def solution(mesh):
    placed = (
        P("rep", "tp"),
        P("tp"),
        P("tp", None),
        P(None, "tp"),
        P("rep", "tp", None),
        P("rep", "tp", None),
        P("rep", "tp", None),
        P("rep", "tp", None),
        P("rep"),
        P("rep"),
        P(),
        P(),
        P(None, "tp"),
        P(None, "tp"),
        P("tp", None),
        P("rep", None),
    )
    return jax.shard_map(
        on_device, mesh=mesh, in_specs=placed, out_specs=P("rep", "tp"), check_vma=False
    )
```

```python
import jax
import jax.numpy as jnp
from jax import lax
from jax.sharding import PartitionSpec as P

HEADS = 36
HDIM = 64
FF = 2880
NEW = 4


EPSILON = 1e-05
BLOCKED = -1e30


def rotate_heads(vectors, places):
    half_dim = HDIM // 2
    frequencies = 10000.0 ** (-jnp.arange(half_dim, dtype=jnp.float32) / half_dim)
    angles = places.astype(jnp.float32)[:, None] * frequencies[None, :]
    cosine = jnp.cos(angles)[:, None, :]
    sine_part = jnp.sin(angles)[:, None, :]
    first = vectors[..., :half_dim]
    second = vectors[..., half_dim:]
    return jnp.concatenate(
        [first * cosine - second * sine_part, second * cosine + first * sine_part], axis=-1
    )


def scale_rows(values, factor):
    row_count, head_count = factor.shape
    return (values.reshape(row_count, head_count, -1) * factor[..., None]).reshape(row_count, -1)


def partner_pairs(count, bit):
    return [(i, i ^ bit) for i in range(count)]


def tp_bits():
    count = lax.axis_size("tp")
    bits = []
    bit = 1
    while bit < count:
        bits.append(bit)
        bit *= 2
    return count, bits


def scatter_sum(values, bits=None):
    count, all_bits = tp_bits()
    bits = all_bits if bits is None else bits
    own_rank = lax.axis_index("tp")
    for bit in bits:
        half = values.shape[1] // 2
        side = (own_rank // bit) % 2
        keep = lax.dynamic_slice_in_dim(values, side * half, half, axis=1)
        send = lax.dynamic_slice_in_dim(values, (1 - side) * half, half, axis=1)
        values = keep + lax.ppermute(send, "tp", partner_pairs(count, bit))
    return values


def gather_cols(values, axis=1, bits=None):
    count, all_bits = tp_bits()
    bits = all_bits if bits is None else bits
    own_rank = lax.axis_index("tp")
    for bit in reversed(bits):
        side = (own_rank // bit) % 2
        other = lax.ppermute(values, "tp", partner_pairs(count, bit))
        values = jnp.where(
            side == 0,
            jnp.concatenate([values, other], axis=axis),
            jnp.concatenate([other, values], axis=axis),
        )
    return values


def kept_position(bits):
    own_rank = lax.axis_index("tp")
    position = 0
    for level, bit in enumerate(bits):
        position = position + ((own_rank // bit) % 2) * 2 ** (len(bits) - 1 - level)
    return position


def exchange_sum(values, bits):
    count, _ = tp_bits()
    for bit in bits:
        values = values + lax.ppermute(values, "tp", partner_pairs(count, bit))
    return values


def exchange_merge(rows, bits):
    count, _ = tp_bits()
    for bit in bits:
        rows = merge_rows(rows, lax.ppermute(rows, "tp", partner_pairs(count, bit)))
    return rows


def merge_rows(first, second):
    joint = jnp.maximum(first[:, -1:], second[:, -1:])
    first_factor = jnp.exp(first[:, -1:] - joint)
    second_factor = jnp.exp(second[:, -1:] - joint)
    body = first[:, :-1] * first_factor + second[:, :-1] * second_factor
    return jnp.concatenate([body, joint], axis=1)


def scatter_merge(rows, bits):
    count, _ = tp_bits()
    own_rank = lax.axis_index("tp")
    for bit in bits:
        half = rows.shape[0] // 2
        side = (own_rank // bit) % 2
        keep = lax.dynamic_slice_in_dim(rows, side * half, half, axis=0)
        send = lax.dynamic_slice_in_dim(rows, (1 - side) * half, half, axis=0)
        rows = merge_rows(keep, lax.ppermute(send, "tp", partner_pairs(count, bit)))
    return rows


def state_rows(peak, total, weighted):
    row_count = peak.shape[0] * peak.shape[1]
    return jnp.concatenate(
        [weighted.reshape(row_count, -1), total.reshape(row_count, 1), peak.reshape(row_count, 1)],
        axis=1,
    )


def exchange_gather(values):
    count = lax.axis_size("tp")
    copies = jnp.broadcast_to(values[None], (count,) + values.shape)
    received = lax.all_to_all(copies, "tp", 0, 0, tiled=True)
    return jnp.transpose(received, (1, 0, 2)).reshape(values.shape[0], -1)


def exchange_scatter_sum(values):
    count = lax.axis_size("tp")
    rows = values.shape[0]
    blocks = jnp.transpose(values.reshape(rows, count, -1), (1, 0, 2))
    received = lax.all_to_all(blocks, "tp", 0, 0, tiled=True)
    return jnp.sum(received, axis=0)


def reverse_blocks(values, count):
    rows, width = values.shape
    levels = count.bit_length() - 1
    split = values.reshape((rows,) + (2,) * levels + (width // count,))
    order = (0,) + tuple(range(levels, 0, -1)) + (levels + 1,)
    return split.transpose(order).reshape(rows, width)


def on_device(
    hidden,
    attn_gain,
    w_qkv,
    w_out,
    prefix_keys,
    prefix_values,
    private_keys,
    private_values,
    group_ids,
    private_lengths,
    moe_gain,
    router,
    w_gate,
    w_up,
    w_down,
    routes,
):
    model_width = w_out.shape[0]
    all_tokens = hidden.shape[0]
    requests = group_ids.shape[0]
    group_count = prefix_keys.shape[0]
    prefix_block = prefix_keys.shape[1]
    private_block = private_keys.shape[1]
    own_rank = lax.axis_index("tp")
    score_scale = HDIM ** (-0.5)
    scaled = (hidden * attn_gain[None, :]).astype(jnp.bfloat16)
    partial_qkv = jnp.dot(scaled, w_qkv, preferred_element_type=jnp.float32)
    own_squares = jnp.sum(hidden * hidden, axis=1)
    qkv_width = partial_qkv.shape[1]
    tp_count = lax.axis_size("tp")
    block = qkv_width // tp_count
    packed = jnp.concatenate(
        [
            partial_qkv.reshape(all_tokens, tp_count, block),
            jnp.broadcast_to(own_squares[:, None, None], (all_tokens, tp_count, 1)),
        ],
        axis=2,
    ).reshape(all_tokens, tp_count * (block + 1))
    _, all_bits = tp_bits()
    near_bits = all_bits[: len(all_bits) // 2]
    far_bits = all_bits[len(all_bits) // 2 :]
    own_block = exchange_sum(scatter_sum(packed, near_bits), far_bits)
    own_block = own_block.reshape(all_tokens, -1, block + 1)
    inv_attn = lax.rsqrt(own_block[:, 0, block] / model_width + EPSILON)
    own_qkv = (inv_attn[:, None, None] * own_block[:, :, :block]).astype(jnp.bfloat16)
    qkv = gather_cols(own_qkv.reshape(all_tokens, -1), bits=near_bits)
    own_lengths = jnp.broadcast_to(private_lengths[:, None], (requests, NEW)).reshape(all_tokens)
    places = (
        prefix_block * lax.axis_size("tp")
        + own_lengths
        + jnp.arange(all_tokens, dtype=jnp.int32) % NEW
    )
    queries = rotate_heads(
        qkv[:, :model_width].astype(jnp.float32).reshape(all_tokens, HEADS, HDIM), places
    ).astype(jnp.bfloat16)
    fresh_keys = rotate_heads(
        qkv[:, model_width : 2 * model_width].astype(jnp.float32).reshape(all_tokens, HEADS, HDIM),
        places,
    ).astype(jnp.bfloat16)
    fresh_values = qkv[:, 2 * model_width :].astype(jnp.float32).reshape(requests, NEW, HEADS, HDIM)
    query_f = queries.astype(jnp.float32).reshape(requests, NEW, HEADS, HDIM)
    pre_keys = prefix_keys.astype(jnp.float32).reshape(group_count, prefix_block, HEADS, HDIM)
    pre_scores = jnp.einsum("rjhd,gphd->rjhgp", query_f, pre_keys) * score_scale
    member = group_ids[:, None] == jnp.arange(group_count, dtype=jnp.int32)[None, :]
    pre_scores = jnp.where(member[:, None, None, :, None], pre_scores, BLOCKED)
    priv_keys = private_keys.astype(jnp.float32).reshape(requests, private_block, HEADS, HDIM)
    priv_scores = jnp.einsum("rjhd,rphd->rjhp", query_f, priv_keys) * score_scale
    slots = own_rank * private_block + jnp.arange(private_block, dtype=jnp.int32)
    live = slots[None, :] < private_lengths[:, None]
    priv_scores = jnp.where(live[:, None, None, :], priv_scores, BLOCKED)
    local_peak = jnp.maximum(jnp.max(pre_scores, axis=(3, 4)), jnp.max(priv_scores, axis=3))
    pre_weights = jnp.exp(pre_scores - local_peak[..., None, None])
    priv_weights = jnp.exp(priv_scores - local_peak[..., None])
    local_total = jnp.sum(pre_weights, axis=(3, 4)) + jnp.sum(priv_weights, axis=3)
    pre_vals = prefix_values.astype(jnp.float32).reshape(group_count, prefix_block, HEADS, HDIM)
    priv_vals = private_values.astype(jnp.float32).reshape(requests, private_block, HEADS, HDIM)
    local_weighted = jnp.einsum("rjhgp,gphd->rjhd", pre_weights, pre_vals) + jnp.einsum(
        "rjhp,rphd->rjhd", priv_weights, priv_vals
    )
    local_peak = local_peak.reshape(all_tokens, HEADS)
    local_total = local_total.reshape(all_tokens, HEADS)
    local_weighted = local_weighted.reshape(all_tokens, model_width)
    cache_rows = scatter_merge(state_rows(local_peak, local_total, local_weighted), near_bits)
    cache_rows = exchange_merge(cache_rows, far_bits)
    key_f = fresh_keys.astype(jnp.float32).reshape(requests, NEW, HEADS, HDIM)
    new_scores = jnp.einsum("rjhd,rihd->rjhi", query_f, key_f) * score_scale
    causal = jnp.arange(NEW)[:, None] >= jnp.arange(NEW)[None, :]
    new_scores = jnp.where(causal[None, :, None, :], new_scores, BLOCKED)
    new_peak = jnp.max(new_scores, axis=3)
    new_weights = jnp.exp(new_scores - new_peak[..., None])
    new_total = jnp.sum(new_weights, axis=3).reshape(all_tokens, HEADS)
    new_weighted = jnp.einsum("rjhi,rihd->rjhd", new_weights, fresh_values).reshape(
        all_tokens, model_width
    )
    new_peak = new_peak.reshape(all_tokens, HEADS)
    new_rows = state_rows(new_peak, new_total, new_weighted)
    own_count = cache_rows.shape[0]
    new_rows = lax.dynamic_slice_in_dim(new_rows, kept_position(near_bits) * own_count, own_count, axis=0)
    final_rows = merge_rows(cache_rows, new_rows)
    attended_rows = (final_rows[:, :HDIM] / final_rows[:, HDIM : HDIM + 1]).astype(jnp.bfloat16)
    attended = gather_cols(attended_rows, axis=0, bits=near_bits).reshape(all_tokens, model_width)
    residual_cols = hidden + jnp.dot(attended, w_out, preferred_element_type=jnp.float32)
    full_rows = exchange_gather(residual_cols)
    inv_norm = lax.rsqrt(jnp.mean(full_rows * full_rows, axis=1) + EPSILON)
    normed = (full_rows * inv_norm[:, None] * moe_gain[None, :]).astype(jnp.bfloat16)
    logits = jnp.dot(normed, router, preferred_element_type=jnp.float32)
    expert_ids = jnp.arange(logits.shape[1], dtype=jnp.int32)
    first_pick = routes[:, 0:1] == expert_ids[None, :]
    second_pick = routes[:, 1:2] == expert_ids[None, :]
    first_logit = jnp.sum(jnp.where(first_pick, logits, 0.0), axis=1)
    second_logit = jnp.sum(jnp.where(second_pick, logits, 0.0), axis=1)
    first_weight = jax.nn.sigmoid(first_logit - second_logit)
    unit_count = w_gate.shape[1]
    own_expert = own_rank * unit_count // FF
    mix_coef = first_weight * (routes[:, 0] == own_expert).astype(jnp.float32) + (
        1.0 - first_weight
    ) * (routes[:, 1] == own_expert).astype(jnp.float32)
    gate_out = jnp.dot(normed, w_gate, preferred_element_type=jnp.float32)
    up_out = jnp.dot(normed, w_up, preferred_element_type=jnp.float32)
    inner_act = (jax.nn.silu(gate_out) * up_out * mix_coef[:, None]).astype(jnp.bfloat16)
    expert_term = jnp.dot(inner_act, w_down, preferred_element_type=jnp.float32)
    return residual_cols + exchange_scatter_sum(expert_term)


def solution(mesh):
    placed = (
        P("rep", "tp"),
        P("tp"),
        P("tp", None),
        P(None, "tp"),
        P("rep", "tp", None),
        P("rep", "tp", None),
        P("rep", "tp", None),
        P("rep", "tp", None),
        P("rep"),
        P("rep"),
        P(),
        P(),
        P(None, "tp"),
        P(None, "tp"),
        P("tp", None),
        P("rep", None),
    )
    return jax.shard_map(
        on_device, mesh=mesh, in_specs=placed, out_specs=P("rep", "tp"), check_vma=False
    )
```

```python
import jax
import jax.numpy as jnp
from jax import lax
from jax.sharding import PartitionSpec as P

HEADS = 36
HDIM = 64
FF = 2880
NEW = 4


EPSILON = 1e-05
BLOCKED = -1e30


def rotate_heads(vectors, places):
    half_dim = HDIM // 2
    frequencies = 10000.0 ** (-jnp.arange(half_dim, dtype=jnp.float32) / half_dim)
    angles = places.astype(jnp.float32)[:, None] * frequencies[None, :]
    cosine = jnp.cos(angles)[:, None, :]
    sine_part = jnp.sin(angles)[:, None, :]
    first = vectors[..., :half_dim]
    second = vectors[..., half_dim:]
    return jnp.concatenate(
        [first * cosine - second * sine_part, second * cosine + first * sine_part], axis=-1
    )


def scale_rows(values, factor):
    row_count, head_count = factor.shape
    return (values.reshape(row_count, head_count, -1) * factor[..., None]).reshape(row_count, -1)


def partner_pairs(count, bit):
    return [(i, i ^ bit) for i in range(count)]


def tp_bits():
    count = lax.axis_size("tp")
    bits = []
    bit = 1
    while bit < count:
        bits.append(bit)
        bit *= 2
    return count, bits


def scatter_sum(values, bits=None):
    count, all_bits = tp_bits()
    bits = all_bits if bits is None else bits
    own_rank = lax.axis_index("tp")
    for bit in bits:
        half = values.shape[1] // 2
        side = (own_rank // bit) % 2
        keep = lax.dynamic_slice_in_dim(values, side * half, half, axis=1)
        send = lax.dynamic_slice_in_dim(values, (1 - side) * half, half, axis=1)
        values = keep + lax.ppermute(send, "tp", partner_pairs(count, bit))
    return values


def gather_cols(values, axis=1, bits=None):
    count, all_bits = tp_bits()
    bits = all_bits if bits is None else bits
    own_rank = lax.axis_index("tp")
    for bit in reversed(bits):
        side = (own_rank // bit) % 2
        other = lax.ppermute(values, "tp", partner_pairs(count, bit))
        values = jnp.where(
            side == 0,
            jnp.concatenate([values, other], axis=axis),
            jnp.concatenate([other, values], axis=axis),
        )
    return values


def kept_position(bits):
    own_rank = lax.axis_index("tp")
    position = 0
    for level, bit in enumerate(bits):
        position = position + ((own_rank // bit) % 2) * 2 ** (len(bits) - 1 - level)
    return position


def exchange_sum(values, bits):
    count, _ = tp_bits()
    for bit in bits:
        values = values + lax.ppermute(values, "tp", partner_pairs(count, bit))
    return values


def exchange_merge(rows, bits):
    count, _ = tp_bits()
    for bit in bits:
        rows = merge_rows(rows, lax.ppermute(rows, "tp", partner_pairs(count, bit)))
    return rows


def merge_rows(first, second):
    joint = jnp.maximum(first[:, -1:], second[:, -1:])
    first_factor = jnp.exp(first[:, -1:] - joint)
    second_factor = jnp.exp(second[:, -1:] - joint)
    body = first[:, :-1] * first_factor + second[:, :-1] * second_factor
    return jnp.concatenate([body, joint], axis=1)


def scatter_merge(rows, bits):
    count, _ = tp_bits()
    own_rank = lax.axis_index("tp")
    for bit in bits:
        half = rows.shape[0] // 2
        side = (own_rank // bit) % 2
        keep = lax.dynamic_slice_in_dim(rows, side * half, half, axis=0)
        send = lax.dynamic_slice_in_dim(rows, (1 - side) * half, half, axis=0)
        rows = merge_rows(keep, lax.ppermute(send, "tp", partner_pairs(count, bit)))
    return rows


def state_rows(peak, total, weighted):
    row_count = peak.shape[0] * peak.shape[1]
    return jnp.concatenate(
        [weighted.reshape(row_count, -1), total.reshape(row_count, 1), peak.reshape(row_count, 1)],
        axis=1,
    )


def exchange_gather(values):
    count = lax.axis_size("tp")
    copies = jnp.broadcast_to(values[None], (count,) + values.shape)
    received = lax.all_to_all(copies, "tp", 0, 0, tiled=True)
    return jnp.transpose(received, (1, 0, 2)).reshape(values.shape[0], -1)


def exchange_scatter_sum(blocks):
    received = lax.all_to_all(blocks, "tp", 0, 0, tiled=True)
    return jnp.sum(received.astype(jnp.float32), axis=0)


def reverse_blocks(values, count):
    rows, width = values.shape
    levels = count.bit_length() - 1
    split = values.reshape((rows,) + (2,) * levels + (width // count,))
    order = (0,) + tuple(range(levels, 0, -1)) + (levels + 1,)
    return split.transpose(order).reshape(rows, width)


def on_device(
    hidden,
    attn_gain,
    w_qkv,
    w_out,
    prefix_keys,
    prefix_values,
    private_keys,
    private_values,
    group_ids,
    private_lengths,
    moe_gain,
    router,
    w_gate,
    w_up,
    w_down,
    routes,
):
    model_width = w_out.shape[0]
    all_tokens = hidden.shape[0]
    requests = group_ids.shape[0]
    group_count = prefix_keys.shape[0]
    prefix_block = prefix_keys.shape[1]
    private_block = private_keys.shape[1]
    own_rank = lax.axis_index("tp")
    score_scale = HDIM ** (-0.5)
    scaled = (hidden * attn_gain[None, :]).astype(jnp.bfloat16)
    partial_qkv = jnp.dot(scaled, w_qkv, preferred_element_type=jnp.float32)
    own_squares = jnp.sum(hidden * hidden, axis=1)
    qkv_width = partial_qkv.shape[1]
    tp_count = lax.axis_size("tp")
    block = qkv_width // tp_count
    packed = jnp.concatenate(
        [
            partial_qkv.reshape(all_tokens, tp_count, block),
            jnp.broadcast_to(own_squares[:, None, None], (all_tokens, tp_count, 1)),
        ],
        axis=2,
    ).reshape(all_tokens, tp_count * (block + 1))
    _, all_bits = tp_bits()
    near_bits = all_bits[: len(all_bits) // 2]
    far_bits = all_bits[len(all_bits) // 2 :]
    own_block = exchange_sum(scatter_sum(packed, near_bits), far_bits)
    own_block = own_block.reshape(all_tokens, -1, block + 1)
    inv_attn = lax.rsqrt(own_block[:, 0, block] / model_width + EPSILON)
    own_qkv = (inv_attn[:, None, None] * own_block[:, :, :block]).astype(jnp.bfloat16)
    qkv = gather_cols(own_qkv.reshape(all_tokens, -1), bits=near_bits)
    own_lengths = jnp.broadcast_to(private_lengths[:, None], (requests, NEW)).reshape(all_tokens)
    places = (
        prefix_block * lax.axis_size("tp")
        + own_lengths
        + jnp.arange(all_tokens, dtype=jnp.int32) % NEW
    )
    queries = rotate_heads(
        qkv[:, :model_width].astype(jnp.float32).reshape(all_tokens, HEADS, HDIM), places
    ).astype(jnp.bfloat16)
    fresh_keys = rotate_heads(
        qkv[:, model_width : 2 * model_width].astype(jnp.float32).reshape(all_tokens, HEADS, HDIM),
        places,
    ).astype(jnp.bfloat16)
    fresh_values = qkv[:, 2 * model_width :].astype(jnp.float32).reshape(requests, NEW, HEADS, HDIM)
    query_f = queries.astype(jnp.float32).reshape(requests, NEW, HEADS, HDIM)
    pre_keys = prefix_keys.astype(jnp.float32).reshape(group_count, prefix_block, HEADS, HDIM)
    pre_scores = jnp.einsum("rjhd,gphd->rjhgp", query_f, pre_keys) * score_scale
    member = group_ids[:, None] == jnp.arange(group_count, dtype=jnp.int32)[None, :]
    pre_scores = jnp.where(member[:, None, None, :, None], pre_scores, BLOCKED)
    priv_keys = private_keys.astype(jnp.float32).reshape(requests, private_block, HEADS, HDIM)
    priv_scores = jnp.einsum("rjhd,rphd->rjhp", query_f, priv_keys) * score_scale
    slots = own_rank * private_block + jnp.arange(private_block, dtype=jnp.int32)
    live = slots[None, :] < private_lengths[:, None]
    priv_scores = jnp.where(live[:, None, None, :], priv_scores, BLOCKED)
    local_peak = jnp.maximum(jnp.max(pre_scores, axis=(3, 4)), jnp.max(priv_scores, axis=3))
    pre_weights = jnp.exp(pre_scores - local_peak[..., None, None])
    priv_weights = jnp.exp(priv_scores - local_peak[..., None])
    local_total = jnp.sum(pre_weights, axis=(3, 4)) + jnp.sum(priv_weights, axis=3)
    pre_vals = prefix_values.astype(jnp.float32).reshape(group_count, prefix_block, HEADS, HDIM)
    priv_vals = private_values.astype(jnp.float32).reshape(requests, private_block, HEADS, HDIM)
    local_weighted = jnp.einsum("rjhgp,gphd->rjhd", pre_weights, pre_vals) + jnp.einsum(
        "rjhp,rphd->rjhd", priv_weights, priv_vals
    )
    local_peak = local_peak.reshape(all_tokens, HEADS)
    local_total = local_total.reshape(all_tokens, HEADS)
    local_weighted = local_weighted.reshape(all_tokens, model_width)
    cache_rows = scatter_merge(state_rows(local_peak, local_total, local_weighted), near_bits)
    cache_rows = exchange_merge(cache_rows, far_bits)
    key_f = fresh_keys.astype(jnp.float32).reshape(requests, NEW, HEADS, HDIM)
    new_scores = jnp.einsum("rjhd,rihd->rjhi", query_f, key_f) * score_scale
    causal = jnp.arange(NEW)[:, None] >= jnp.arange(NEW)[None, :]
    new_scores = jnp.where(causal[None, :, None, :], new_scores, BLOCKED)
    new_peak = jnp.max(new_scores, axis=3)
    new_weights = jnp.exp(new_scores - new_peak[..., None])
    new_total = jnp.sum(new_weights, axis=3).reshape(all_tokens, HEADS)
    new_weighted = jnp.einsum("rjhi,rihd->rjhd", new_weights, fresh_values).reshape(
        all_tokens, model_width
    )
    new_peak = new_peak.reshape(all_tokens, HEADS)
    new_rows = state_rows(new_peak, new_total, new_weighted)
    own_count = cache_rows.shape[0]
    new_rows = lax.dynamic_slice_in_dim(new_rows, kept_position(near_bits) * own_count, own_count, axis=0)
    final_rows = merge_rows(cache_rows, new_rows)
    attended_rows = (final_rows[:, :HDIM] / final_rows[:, HDIM : HDIM + 1]).astype(jnp.bfloat16)
    attended = gather_cols(attended_rows, axis=0, bits=near_bits).reshape(all_tokens, model_width)
    residual_cols = hidden + jnp.dot(attended, w_out, preferred_element_type=jnp.float32)
    full_rows = exchange_gather(residual_cols.astype(jnp.bfloat16)).astype(jnp.float32)
    inv_norm = lax.rsqrt(jnp.mean(full_rows * full_rows, axis=1) + EPSILON)
    normed = (full_rows * inv_norm[:, None] * moe_gain[None, :]).astype(jnp.bfloat16)
    logits = jnp.dot(normed, router, preferred_element_type=jnp.float32)
    expert_ids = jnp.arange(logits.shape[1], dtype=jnp.int32)
    first_pick = routes[:, 0:1] == expert_ids[None, :]
    second_pick = routes[:, 1:2] == expert_ids[None, :]
    first_logit = jnp.sum(jnp.where(first_pick, logits, 0.0), axis=1)
    second_logit = jnp.sum(jnp.where(second_pick, logits, 0.0), axis=1)
    first_weight = jax.nn.sigmoid(first_logit - second_logit)
    unit_count = w_gate.shape[1]
    own_expert = own_rank * unit_count // FF
    mix_coef = first_weight * (routes[:, 0] == own_expert).astype(jnp.float32) + (
        1.0 - first_weight
    ) * (routes[:, 1] == own_expert).astype(jnp.float32)
    gate_out = jnp.dot(normed, w_gate, preferred_element_type=jnp.float32)
    up_out = jnp.dot(normed, w_up, preferred_element_type=jnp.float32)
    inner_act = (jax.nn.silu(gate_out) * up_out * mix_coef[:, None]).astype(jnp.bfloat16)
    expert_blocks = jnp.einsum(
        "tf,fbc->btc",
        inner_act,
        w_down.reshape(w_down.shape[0], tp_count, -1),
        preferred_element_type=jnp.float32,
    )
    return residual_cols + exchange_scatter_sum(expert_blocks.astype(jnp.bfloat16))


def solution(mesh):
    placed = (
        P("rep", "tp"),
        P("tp"),
        P("tp", None),
        P(None, "tp"),
        P("rep", "tp", None),
        P("rep", "tp", None),
        P("rep", "tp", None),
        P("rep", "tp", None),
        P("rep"),
        P("rep"),
        P(),
        P(),
        P(None, "tp"),
        P(None, "tp"),
        P("tp", None),
        P("rep", None),
    )
    return jax.shard_map(
        on_device, mesh=mesh, in_specs=placed, out_specs=P("rep", "tp"), check_vma=False
    )
```

```python
import jax
import jax.numpy as jnp
from jax import lax
from jax.sharding import PartitionSpec as P

HEADS = 36
HDIM = 64
FF = 2880
NEW = 4


EPSILON = 1e-05
BLOCKED = -1e30


def rotate_heads(vectors, places):
    half_dim = HDIM // 2
    frequencies = 10000.0 ** (-jnp.arange(half_dim, dtype=jnp.float32) / half_dim)
    angles = places.astype(jnp.float32)[:, None] * frequencies[None, :]
    cosine = jnp.cos(angles)[:, None, :]
    sine_part = jnp.sin(angles)[:, None, :]
    first = vectors[..., :half_dim]
    second = vectors[..., half_dim:]
    return jnp.concatenate(
        [first * cosine - second * sine_part, second * cosine + first * sine_part], axis=-1
    )


def scale_rows(values, factor):
    row_count, head_count = factor.shape
    return (values.reshape(row_count, head_count, -1) * factor[..., None]).reshape(row_count, -1)


def partner_pairs(count, bit):
    return [(i, i ^ bit) for i in range(count)]


def tp_bits():
    count = lax.axis_size("tp")
    bits = []
    bit = 1
    while bit < count:
        bits.append(bit)
        bit *= 2
    return count, bits


def scatter_sum(values, bits=None):
    count, all_bits = tp_bits()
    bits = all_bits if bits is None else bits
    own_rank = lax.axis_index("tp")
    for bit in bits:
        half = values.shape[1] // 2
        side = (own_rank // bit) % 2
        keep = lax.dynamic_slice_in_dim(values, side * half, half, axis=1)
        send = lax.dynamic_slice_in_dim(values, (1 - side) * half, half, axis=1)
        values = keep + lax.ppermute(send, "tp", partner_pairs(count, bit))
    return values


def gather_cols(values, axis=1, bits=None):
    count, all_bits = tp_bits()
    bits = all_bits if bits is None else bits
    own_rank = lax.axis_index("tp")
    for bit in reversed(bits):
        side = (own_rank // bit) % 2
        other = lax.ppermute(values, "tp", partner_pairs(count, bit))
        values = jnp.where(
            side == 0,
            jnp.concatenate([values, other], axis=axis),
            jnp.concatenate([other, values], axis=axis),
        )
    return values


def kept_position(bits):
    own_rank = lax.axis_index("tp")
    position = 0
    for level, bit in enumerate(bits):
        position = position + ((own_rank // bit) % 2) * 2 ** (len(bits) - 1 - level)
    return position


def exchange_sum(values, bits):
    count, _ = tp_bits()
    for bit in bits:
        values = values + lax.ppermute(values, "tp", partner_pairs(count, bit))
    return values


def exchange_merge(rows, bits):
    count, _ = tp_bits()
    for bit in bits:
        rows = merge_rows(rows, lax.ppermute(rows, "tp", partner_pairs(count, bit)))
    return rows


def merge_rows(first, second):
    joint = jnp.maximum(first[:, -1:], second[:, -1:])
    first_factor = jnp.exp(first[:, -1:] - joint)
    second_factor = jnp.exp(second[:, -1:] - joint)
    body = first[:, :-1] * first_factor + second[:, :-1] * second_factor
    return jnp.concatenate([body, joint], axis=1)


def scatter_merge(rows, bits):
    count, _ = tp_bits()
    own_rank = lax.axis_index("tp")
    for bit in bits:
        half = rows.shape[0] // 2
        side = (own_rank // bit) % 2
        keep = lax.dynamic_slice_in_dim(rows, side * half, half, axis=0)
        send = lax.dynamic_slice_in_dim(rows, (1 - side) * half, half, axis=0)
        rows = merge_rows(keep, lax.ppermute(send, "tp", partner_pairs(count, bit)))
    return rows


def state_rows(peak, total, weighted):
    row_count = peak.shape[0] * peak.shape[1]
    return jnp.concatenate(
        [weighted.reshape(row_count, -1), total.reshape(row_count, 1), peak.reshape(row_count, 1)],
        axis=1,
    )


def exchange_gather(values):
    count = lax.axis_size("tp")
    copies = jnp.broadcast_to(values[None], (count,) + values.shape)
    received = lax.all_to_all(copies, "tp", 0, 0, tiled=True)
    return jnp.transpose(received, (1, 0, 2)).reshape(values.shape[0], -1)


def exchange_scatter_sum(blocks):
    received = lax.all_to_all(blocks, "tp", 0, 0, tiled=True)
    return jnp.sum(received.astype(jnp.float32), axis=0)


def spread_requests(values, bits):
    count, _ = tp_bits()
    own_rank = lax.axis_index("tp")
    for step, bit in enumerate(reversed(bits)):
        side = (own_rank // bit) % 2
        held, tokens, width = values.shape
        split = values.reshape(held // 2, 2, tokens, width)
        keep = lax.dynamic_index_in_dim(split, side, axis=1, keepdims=False)
        send = lax.dynamic_index_in_dim(split, 1 - side, axis=1, keepdims=False)
        other = lax.ppermute(send, "tp", partner_pairs(count, bit))
        values = jnp.where(
            side == 0,
            jnp.concatenate([keep, other], axis=2),
            jnp.concatenate([other, keep], axis=2),
        )
    return values


def reverse_blocks(values, count):
    rows, width = values.shape
    levels = count.bit_length() - 1
    split = values.reshape((rows,) + (2,) * levels + (width // count,))
    order = (0,) + tuple(range(levels, 0, -1)) + (levels + 1,)
    return split.transpose(order).reshape(rows, width)


def on_device(
    hidden,
    attn_gain,
    w_qkv,
    w_out,
    prefix_keys,
    prefix_values,
    private_keys,
    private_values,
    group_ids,
    private_lengths,
    moe_gain,
    router,
    w_gate,
    w_up,
    w_down,
    routes,
):
    model_width = w_out.shape[0]
    all_tokens = hidden.shape[0]
    requests = group_ids.shape[0]
    group_count = prefix_keys.shape[0]
    prefix_block = prefix_keys.shape[1]
    private_block = private_keys.shape[1]
    own_rank = lax.axis_index("tp")
    score_scale = HDIM ** (-0.5)
    scaled = (hidden * attn_gain[None, :]).astype(jnp.bfloat16)
    partial_qkv = jnp.dot(scaled, w_qkv, preferred_element_type=jnp.float32)
    own_squares = jnp.sum(hidden * hidden, axis=1)
    tp_count = lax.axis_size("tp")
    query_block = model_width // tp_count
    kv_block = 2 * model_width // tp_count
    block = query_block + kv_block
    packed = jnp.concatenate(
        [
            partial_qkv[:, :model_width].reshape(all_tokens, tp_count, query_block),
            partial_qkv[:, model_width:].reshape(all_tokens, tp_count, kv_block),
            jnp.broadcast_to(own_squares[:, None, None], (all_tokens, tp_count, 1)),
        ],
        axis=2,
    ).reshape(all_tokens, tp_count * (block + 1))
    _, all_bits = tp_bits()
    near_bits = all_bits[: len(all_bits) // 2]
    far_bits = all_bits[len(all_bits) // 2 :]
    assert 2 ** len(near_bits) == requests
    own_block = exchange_sum(scatter_sum(packed, near_bits), far_bits)
    own_block = own_block.reshape(all_tokens, -1, block + 1)
    inv_attn = lax.rsqrt(own_block[:, 0, block] / model_width + EPSILON)
    own_qkv = (inv_attn[:, None, None] * own_block[:, :, :block]).astype(jnp.bfloat16)
    query_cols = gather_cols(own_qkv[:, :, :query_block].reshape(all_tokens, -1), bits=near_bits)
    own_kv = own_qkv[:, :, query_block:].reshape(requests, NEW, -1)
    own_request = kept_position(near_bits)
    request_kv = spread_requests(own_kv, near_bits).reshape(NEW, 2 * model_width)
    own_lengths = jnp.broadcast_to(private_lengths[:, None], (requests, NEW)).reshape(all_tokens)
    places = (
        prefix_block * lax.axis_size("tp")
        + own_lengths
        + jnp.arange(all_tokens, dtype=jnp.int32) % NEW
    )
    queries = rotate_heads(
        query_cols.astype(jnp.float32).reshape(all_tokens, HEADS, HDIM), places
    ).astype(jnp.bfloat16)
    request_places = lax.dynamic_slice_in_dim(places, own_request * NEW, NEW)
    fresh_keys = rotate_heads(
        request_kv[:, :model_width].astype(jnp.float32).reshape(NEW, HEADS, HDIM),
        request_places,
    ).astype(jnp.bfloat16)
    fresh_values = request_kv[:, model_width:].astype(jnp.float32).reshape(NEW, HEADS, HDIM)
    query_f = queries.astype(jnp.float32).reshape(requests, NEW, HEADS, HDIM)
    pre_keys = prefix_keys.astype(jnp.float32).reshape(group_count, prefix_block, HEADS, HDIM)
    pre_scores = jnp.einsum("rjhd,gphd->rjhgp", query_f, pre_keys) * score_scale
    member = group_ids[:, None] == jnp.arange(group_count, dtype=jnp.int32)[None, :]
    pre_scores = jnp.where(member[:, None, None, :, None], pre_scores, BLOCKED)
    priv_keys = private_keys.astype(jnp.float32).reshape(requests, private_block, HEADS, HDIM)
    priv_scores = jnp.einsum("rjhd,rphd->rjhp", query_f, priv_keys) * score_scale
    slots = own_rank * private_block + jnp.arange(private_block, dtype=jnp.int32)
    live = slots[None, :] < private_lengths[:, None]
    priv_scores = jnp.where(live[:, None, None, :], priv_scores, BLOCKED)
    local_peak = jnp.maximum(jnp.max(pre_scores, axis=(3, 4)), jnp.max(priv_scores, axis=3))
    pre_weights = jnp.exp(pre_scores - local_peak[..., None, None])
    priv_weights = jnp.exp(priv_scores - local_peak[..., None])
    local_total = jnp.sum(pre_weights, axis=(3, 4)) + jnp.sum(priv_weights, axis=3)
    pre_vals = prefix_values.astype(jnp.float32).reshape(group_count, prefix_block, HEADS, HDIM)
    priv_vals = private_values.astype(jnp.float32).reshape(requests, private_block, HEADS, HDIM)
    local_weighted = jnp.einsum("rjhgp,gphd->rjhd", pre_weights, pre_vals) + jnp.einsum(
        "rjhp,rphd->rjhd", priv_weights, priv_vals
    )
    local_peak = local_peak.reshape(all_tokens, HEADS)
    local_total = local_total.reshape(all_tokens, HEADS)
    local_weighted = local_weighted.reshape(all_tokens, model_width)
    cache_rows = scatter_merge(state_rows(local_peak, local_total, local_weighted), near_bits)
    cache_rows = exchange_merge(cache_rows, far_bits)
    request_query = lax.dynamic_index_in_dim(query_f, own_request, axis=0, keepdims=False)
    key_f = fresh_keys.astype(jnp.float32)
    new_scores = jnp.einsum("jhd,ihd->jhi", request_query, key_f) * score_scale
    causal = jnp.arange(NEW)[:, None] >= jnp.arange(NEW)[None, :]
    new_scores = jnp.where(causal[:, None, :], new_scores, BLOCKED)
    new_peak = jnp.max(new_scores, axis=2)
    new_weights = jnp.exp(new_scores - new_peak[..., None])
    new_total = jnp.sum(new_weights, axis=2)
    new_weighted = jnp.einsum("jhi,ihd->jhd", new_weights, fresh_values)
    new_rows = state_rows(new_peak, new_total, new_weighted)
    final_rows = merge_rows(cache_rows, new_rows)
    attended_rows = (final_rows[:, :HDIM] / final_rows[:, HDIM : HDIM + 1]).astype(jnp.bfloat16)
    attended = gather_cols(attended_rows, axis=0, bits=near_bits).reshape(all_tokens, model_width)
    residual_cols = hidden + jnp.dot(attended, w_out, preferred_element_type=jnp.float32)
    full_rows = exchange_gather(residual_cols.astype(jnp.bfloat16)).astype(jnp.float32)
    inv_norm = lax.rsqrt(jnp.mean(full_rows * full_rows, axis=1) + EPSILON)
    normed = (full_rows * inv_norm[:, None] * moe_gain[None, :]).astype(jnp.bfloat16)
    logits = jnp.dot(normed, router, preferred_element_type=jnp.float32)
    expert_ids = jnp.arange(logits.shape[1], dtype=jnp.int32)
    first_pick = routes[:, 0:1] == expert_ids[None, :]
    second_pick = routes[:, 1:2] == expert_ids[None, :]
    first_logit = jnp.sum(jnp.where(first_pick, logits, 0.0), axis=1)
    second_logit = jnp.sum(jnp.where(second_pick, logits, 0.0), axis=1)
    first_weight = jax.nn.sigmoid(first_logit - second_logit)
    unit_count = w_gate.shape[1]
    own_expert = own_rank * unit_count // FF
    mix_coef = first_weight * (routes[:, 0] == own_expert).astype(jnp.float32) + (
        1.0 - first_weight
    ) * (routes[:, 1] == own_expert).astype(jnp.float32)
    gate_out = jnp.dot(normed, w_gate, preferred_element_type=jnp.float32)
    up_out = jnp.dot(normed, w_up, preferred_element_type=jnp.float32)
    inner_act = (jax.nn.silu(gate_out) * up_out * mix_coef[:, None]).astype(jnp.bfloat16)
    expert_blocks = jnp.einsum(
        "tf,fbc->btc",
        inner_act,
        w_down.reshape(w_down.shape[0], tp_count, -1),
        preferred_element_type=jnp.float32,
    )
    return residual_cols + exchange_scatter_sum(expert_blocks.astype(jnp.bfloat16))


def solution(mesh):
    placed = (
        P("rep", "tp"),
        P("tp"),
        P("tp", None),
        P(None, "tp"),
        P("rep", "tp", None),
        P("rep", "tp", None),
        P("rep", "tp", None),
        P("rep", "tp", None),
        P("rep"),
        P("rep"),
        P(),
        P(),
        P(None, "tp"),
        P(None, "tp"),
        P("tp", None),
        P("rep", None),
    )
    return jax.shard_map(
        on_device, mesh=mesh, in_specs=placed, out_specs=P("rep", "tp"), check_vma=False
    )
```

```python
import jax
import jax.numpy as jnp
from jax import lax
from jax.sharding import PartitionSpec as P

HEADS = 36
HDIM = 64
FF = 2880
NEW = 4


EPSILON = 1e-05
BLOCKED = -1e30


def rotate_heads(vectors, places):
    half_dim = HDIM // 2
    frequencies = 10000.0 ** (-jnp.arange(half_dim, dtype=jnp.float32) / half_dim)
    angles = places.astype(jnp.float32)[:, None] * frequencies[None, :]
    cosine = jnp.cos(angles)[:, None, :]
    sine_part = jnp.sin(angles)[:, None, :]
    first = vectors[..., :half_dim]
    second = vectors[..., half_dim:]
    return jnp.concatenate(
        [first * cosine - second * sine_part, second * cosine + first * sine_part], axis=-1
    )


def scale_rows(values, factor):
    row_count, head_count = factor.shape
    return (values.reshape(row_count, head_count, -1) * factor[..., None]).reshape(row_count, -1)


def partner_pairs(count, bit):
    return [(i, i ^ bit) for i in range(count)]


def tp_bits():
    count = lax.axis_size("tp")
    bits = []
    bit = 1
    while bit < count:
        bits.append(bit)
        bit *= 2
    return count, bits


def scatter_sum(values, bits=None):
    count, all_bits = tp_bits()
    bits = all_bits if bits is None else bits
    own_rank = lax.axis_index("tp")
    for bit in bits:
        half = values.shape[1] // 2
        side = (own_rank // bit) % 2
        keep = lax.dynamic_slice_in_dim(values, side * half, half, axis=1)
        send = lax.dynamic_slice_in_dim(values, (1 - side) * half, half, axis=1)
        values = keep + lax.ppermute(send, "tp", partner_pairs(count, bit))
    return values


def gather_cols(values, axis=1, bits=None):
    count, all_bits = tp_bits()
    bits = all_bits if bits is None else bits
    own_rank = lax.axis_index("tp")
    for bit in reversed(bits):
        side = (own_rank // bit) % 2
        other = lax.ppermute(values, "tp", partner_pairs(count, bit))
        values = jnp.where(
            side == 0,
            jnp.concatenate([values, other], axis=axis),
            jnp.concatenate([other, values], axis=axis),
        )
    return values


def kept_position(bits):
    own_rank = lax.axis_index("tp")
    position = 0
    for level, bit in enumerate(bits):
        position = position + ((own_rank // bit) % 2) * 2 ** (len(bits) - 1 - level)
    return position


def exchange_sum(values, bits):
    count, _ = tp_bits()
    for bit in bits:
        values = values + lax.ppermute(values, "tp", partner_pairs(count, bit))
    return values


def exchange_merge(rows, bits):
    count, _ = tp_bits()
    for bit in bits:
        rows = merge_rows(rows, lax.ppermute(rows, "tp", partner_pairs(count, bit)))
    return rows


def merge_rows(first, second):
    joint = jnp.maximum(first[:, -1:], second[:, -1:])
    first_factor = jnp.exp(first[:, -1:] - joint)
    second_factor = jnp.exp(second[:, -1:] - joint)
    body = first[:, :-1] * first_factor + second[:, :-1] * second_factor
    return jnp.concatenate([body, joint], axis=1)


def scatter_merge(rows, bits):
    count, _ = tp_bits()
    own_rank = lax.axis_index("tp")
    for bit in bits:
        half = rows.shape[0] // 2
        side = (own_rank // bit) % 2
        keep = lax.dynamic_slice_in_dim(rows, side * half, half, axis=0)
        send = lax.dynamic_slice_in_dim(rows, (1 - side) * half, half, axis=0)
        rows = merge_rows(keep, lax.ppermute(send, "tp", partner_pairs(count, bit)))
    return rows


def state_rows(peak, total, weighted):
    row_count = peak.shape[0] * peak.shape[1]
    return jnp.concatenate(
        [weighted.reshape(row_count, -1), total.reshape(row_count, 1), peak.reshape(row_count, 1)],
        axis=1,
    )


def exchange_gather(values):
    count = lax.axis_size("tp")
    copies = jnp.broadcast_to(values[None], (count,) + values.shape)
    received = lax.all_to_all(copies, "tp", 0, 0, tiled=True)
    return jnp.transpose(received, (1, 0, 2)).reshape(values.shape[0], -1)


def exchange_scatter_sum(blocks):
    received = lax.all_to_all(blocks, "tp", 0, 0, tiled=True)
    return jnp.sum(received.astype(jnp.float32), axis=0)


def gather_and_spread(queries, kv, bits):
    count, _ = tp_bits()
    own_rank = lax.axis_index("tp")
    query_rows, _ = queries.shape
    for bit in reversed(bits):
        side = (own_rank // bit) % 2
        held, tokens, width = kv.shape
        split = kv.reshape(held // 2, 2, tokens, width)
        keep = lax.dynamic_index_in_dim(split, side, axis=1, keepdims=False)
        send = lax.dynamic_index_in_dim(split, 1 - side, axis=1, keepdims=False)
        query_width = queries.shape[1]
        payload = jnp.concatenate([queries, send.reshape(query_rows, -1)], axis=1)
        other = lax.ppermute(payload, "tp", partner_pairs(count, bit))
        other_queries = other[:, :query_width]
        other_kv = other[:, query_width:].reshape(send.shape)
        queries = jnp.where(
            side == 0,
            jnp.concatenate([queries, other_queries], axis=1),
            jnp.concatenate([other_queries, queries], axis=1),
        )
        kv = jnp.where(
            side == 0,
            jnp.concatenate([keep, other_kv], axis=2),
            jnp.concatenate([other_kv, keep], axis=2),
        )
    return queries, kv


def reverse_blocks(values, count):
    rows, width = values.shape
    levels = count.bit_length() - 1
    split = values.reshape((rows,) + (2,) * levels + (width // count,))
    order = (0,) + tuple(range(levels, 0, -1)) + (levels + 1,)
    return split.transpose(order).reshape(rows, width)


def on_device(
    hidden,
    attn_gain,
    w_qkv,
    w_out,
    prefix_keys,
    prefix_values,
    private_keys,
    private_values,
    group_ids,
    private_lengths,
    moe_gain,
    router,
    w_gate,
    w_up,
    w_down,
    routes,
):
    model_width = w_out.shape[0]
    all_tokens = hidden.shape[0]
    requests = group_ids.shape[0]
    group_count = prefix_keys.shape[0]
    prefix_block = prefix_keys.shape[1]
    private_block = private_keys.shape[1]
    own_rank = lax.axis_index("tp")
    score_scale = HDIM ** (-0.5)
    scaled = (hidden * attn_gain[None, :]).astype(jnp.bfloat16)
    partial_qkv = jnp.dot(scaled, w_qkv, preferred_element_type=jnp.float32)
    own_squares = jnp.sum(hidden * hidden, axis=1)
    tp_count = lax.axis_size("tp")
    query_block = model_width // tp_count
    kv_block = 2 * model_width // tp_count
    block = query_block + kv_block
    packed = jnp.concatenate(
        [
            partial_qkv[:, :model_width].reshape(all_tokens, tp_count, query_block),
            partial_qkv[:, model_width:].reshape(all_tokens, tp_count, kv_block),
            jnp.broadcast_to(own_squares[:, None, None], (all_tokens, tp_count, 1)),
        ],
        axis=2,
    ).reshape(all_tokens, tp_count * (block + 1))
    _, all_bits = tp_bits()
    near_bits = all_bits[: len(all_bits) // 2]
    far_bits = all_bits[len(all_bits) // 2 :]
    assert 2 ** len(near_bits) == requests
    own_block = exchange_sum(scatter_sum(packed, near_bits), far_bits)
    own_block = own_block.reshape(all_tokens, -1, block + 1)
    inv_attn = lax.rsqrt(own_block[:, 0, block] / model_width + EPSILON)
    own_qkv = (inv_attn[:, None, None] * own_block[:, :, :block]).astype(jnp.bfloat16)
    own_kv = own_qkv[:, :, query_block:].reshape(requests, NEW, -1)
    own_request = kept_position(near_bits)
    query_cols, request_kv = gather_and_spread(
        own_qkv[:, :, :query_block].reshape(all_tokens, -1), own_kv, near_bits
    )
    request_kv = request_kv.reshape(NEW, 2 * model_width)
    own_lengths = jnp.broadcast_to(private_lengths[:, None], (requests, NEW)).reshape(all_tokens)
    places = (
        prefix_block * lax.axis_size("tp")
        + own_lengths
        + jnp.arange(all_tokens, dtype=jnp.int32) % NEW
    )
    queries = rotate_heads(
        query_cols.astype(jnp.float32).reshape(all_tokens, HEADS, HDIM), places
    ).astype(jnp.bfloat16)
    request_places = lax.dynamic_slice_in_dim(places, own_request * NEW, NEW)
    fresh_keys = rotate_heads(
        request_kv[:, :model_width].astype(jnp.float32).reshape(NEW, HEADS, HDIM),
        request_places,
    ).astype(jnp.bfloat16)
    fresh_values = request_kv[:, model_width:].astype(jnp.float32).reshape(NEW, HEADS, HDIM)
    query_f = queries.astype(jnp.float32).reshape(requests, NEW, HEADS, HDIM)
    pre_keys = prefix_keys.astype(jnp.float32).reshape(group_count, prefix_block, HEADS, HDIM)
    pre_scores = jnp.einsum("rjhd,gphd->rjhgp", query_f, pre_keys) * score_scale
    member = group_ids[:, None] == jnp.arange(group_count, dtype=jnp.int32)[None, :]
    pre_scores = jnp.where(member[:, None, None, :, None], pre_scores, BLOCKED)
    priv_keys = private_keys.astype(jnp.float32).reshape(requests, private_block, HEADS, HDIM)
    priv_scores = jnp.einsum("rjhd,rphd->rjhp", query_f, priv_keys) * score_scale
    slots = own_rank * private_block + jnp.arange(private_block, dtype=jnp.int32)
    live = slots[None, :] < private_lengths[:, None]
    priv_scores = jnp.where(live[:, None, None, :], priv_scores, BLOCKED)
    local_peak = jnp.maximum(jnp.max(pre_scores, axis=(3, 4)), jnp.max(priv_scores, axis=3))
    pre_weights = jnp.exp(pre_scores - local_peak[..., None, None])
    priv_weights = jnp.exp(priv_scores - local_peak[..., None])
    local_total = jnp.sum(pre_weights, axis=(3, 4)) + jnp.sum(priv_weights, axis=3)
    pre_vals = prefix_values.astype(jnp.float32).reshape(group_count, prefix_block, HEADS, HDIM)
    priv_vals = private_values.astype(jnp.float32).reshape(requests, private_block, HEADS, HDIM)
    local_weighted = jnp.einsum("rjhgp,gphd->rjhd", pre_weights, pre_vals) + jnp.einsum(
        "rjhp,rphd->rjhd", priv_weights, priv_vals
    )
    local_peak = local_peak.reshape(all_tokens, HEADS)
    local_total = local_total.reshape(all_tokens, HEADS)
    local_weighted = local_weighted.reshape(all_tokens, model_width)
    cache_rows = scatter_merge(state_rows(local_peak, local_total, local_weighted), near_bits)
    cache_rows = exchange_merge(cache_rows, far_bits)
    request_query = lax.dynamic_index_in_dim(query_f, own_request, axis=0, keepdims=False)
    key_f = fresh_keys.astype(jnp.float32)
    new_scores = jnp.einsum("jhd,ihd->jhi", request_query, key_f) * score_scale
    causal = jnp.arange(NEW)[:, None] >= jnp.arange(NEW)[None, :]
    new_scores = jnp.where(causal[:, None, :], new_scores, BLOCKED)
    new_peak = jnp.max(new_scores, axis=2)
    new_weights = jnp.exp(new_scores - new_peak[..., None])
    new_total = jnp.sum(new_weights, axis=2)
    new_weighted = jnp.einsum("jhi,ihd->jhd", new_weights, fresh_values)
    new_rows = state_rows(new_peak, new_total, new_weighted)
    final_rows = merge_rows(cache_rows, new_rows)
    attended_rows = (final_rows[:, :HDIM] / final_rows[:, HDIM : HDIM + 1]).astype(jnp.bfloat16)
    attended = gather_cols(attended_rows, axis=0, bits=near_bits).reshape(all_tokens, model_width)
    residual_cols = hidden + jnp.dot(attended, w_out, preferred_element_type=jnp.float32)
    full_rows = exchange_gather(residual_cols.astype(jnp.bfloat16)).astype(jnp.float32)
    inv_norm = lax.rsqrt(jnp.mean(full_rows * full_rows, axis=1) + EPSILON)
    normed = (full_rows * inv_norm[:, None] * moe_gain[None, :]).astype(jnp.bfloat16)
    logits = jnp.dot(normed, router, preferred_element_type=jnp.float32)
    expert_ids = jnp.arange(logits.shape[1], dtype=jnp.int32)
    first_pick = routes[:, 0:1] == expert_ids[None, :]
    second_pick = routes[:, 1:2] == expert_ids[None, :]
    first_logit = jnp.sum(jnp.where(first_pick, logits, 0.0), axis=1)
    second_logit = jnp.sum(jnp.where(second_pick, logits, 0.0), axis=1)
    first_weight = jax.nn.sigmoid(first_logit - second_logit)
    unit_count = w_gate.shape[1]
    own_expert = own_rank * unit_count // FF
    mix_coef = first_weight * (routes[:, 0] == own_expert).astype(jnp.float32) + (
        1.0 - first_weight
    ) * (routes[:, 1] == own_expert).astype(jnp.float32)
    gate_out = jnp.dot(normed, w_gate, preferred_element_type=jnp.float32)
    up_out = jnp.dot(normed, w_up, preferred_element_type=jnp.float32)
    inner_act = (jax.nn.silu(gate_out) * up_out * mix_coef[:, None]).astype(jnp.bfloat16)
    expert_blocks = jnp.einsum(
        "tf,fbc->btc",
        inner_act,
        w_down.reshape(w_down.shape[0], tp_count, -1),
        preferred_element_type=jnp.float32,
    )
    return residual_cols + exchange_scatter_sum(expert_blocks.astype(jnp.bfloat16))


def solution(mesh):
    placed = (
        P("rep", "tp"),
        P("tp"),
        P("tp", None),
        P(None, "tp"),
        P("rep", "tp", None),
        P("rep", "tp", None),
        P("rep", "tp", None),
        P("rep", "tp", None),
        P("rep"),
        P("rep"),
        P(),
        P(),
        P(None, "tp"),
        P(None, "tp"),
        P("tp", None),
        P("rep", None),
    )
    return jax.shard_map(
        on_device, mesh=mesh, in_specs=placed, out_specs=P("rep", "tp"), check_vma=False
    )
```

```python
import jax
import jax.numpy as jnp
from jax import lax
from jax.sharding import PartitionSpec as P

HEADS = 36
HDIM = 64
FF = 2880
NEW = 4


EPSILON = 1e-05
BLOCKED = -1e30


def rotate_heads(vectors, places):
    half_dim = HDIM // 2
    frequencies = 10000.0 ** (-jnp.arange(half_dim, dtype=jnp.float32) / half_dim)
    angles = places.astype(jnp.float32)[:, None] * frequencies[None, :]
    cosine = jnp.cos(angles)[:, None, :]
    sine_part = jnp.sin(angles)[:, None, :]
    first = vectors[..., :half_dim]
    second = vectors[..., half_dim:]
    return jnp.concatenate(
        [first * cosine - second * sine_part, second * cosine + first * sine_part], axis=-1
    )


def scale_rows(values, factor):
    row_count, head_count = factor.shape
    return (values.reshape(row_count, head_count, -1) * factor[..., None]).reshape(row_count, -1)


def partner_pairs(count, bit):
    return [(i, i ^ bit) for i in range(count)]


def tp_bits():
    count = lax.axis_size("tp")
    bits = []
    bit = 1
    while bit < count:
        bits.append(bit)
        bit *= 2
    return count, bits


def scatter_sum(values, bits=None):
    count, all_bits = tp_bits()
    bits = all_bits if bits is None else bits
    own_rank = lax.axis_index("tp")
    for bit in bits:
        half = values.shape[1] // 2
        side = (own_rank // bit) % 2
        keep = lax.dynamic_slice_in_dim(values, side * half, half, axis=1)
        send = lax.dynamic_slice_in_dim(values, (1 - side) * half, half, axis=1)
        values = keep + lax.ppermute(send, "tp", partner_pairs(count, bit))
    return values


def gather_cols(values, axis=1, bits=None):
    count, all_bits = tp_bits()
    bits = all_bits if bits is None else bits
    own_rank = lax.axis_index("tp")
    for bit in reversed(bits):
        side = (own_rank // bit) % 2
        other = lax.ppermute(values, "tp", partner_pairs(count, bit))
        values = jnp.where(
            side == 0,
            jnp.concatenate([values, other], axis=axis),
            jnp.concatenate([other, values], axis=axis),
        )
    return values


def kept_position(bits):
    own_rank = lax.axis_index("tp")
    position = 0
    for level, bit in enumerate(bits):
        position = position + ((own_rank // bit) % 2) * 2 ** (len(bits) - 1 - level)
    return position


def exchange_sum(values, bits):
    count, _ = tp_bits()
    for bit in bits:
        values = values + lax.ppermute(values, "tp", partner_pairs(count, bit))
    return values


def exchange_merge(rows, bits):
    count, _ = tp_bits()
    for bit in bits:
        rows = merge_rows(rows, lax.ppermute(rows, "tp", partner_pairs(count, bit)))
    return rows


def merge_rows(first, second):
    joint = jnp.maximum(first[:, -1:], second[:, -1:])
    first_factor = jnp.exp(first[:, -1:] - joint)
    second_factor = jnp.exp(second[:, -1:] - joint)
    body = first[:, :-1] * first_factor + second[:, :-1] * second_factor
    return jnp.concatenate([body, joint], axis=1)


def scatter_merge(rows, bits):
    count, _ = tp_bits()
    own_rank = lax.axis_index("tp")
    for bit in bits:
        half = rows.shape[0] // 2
        side = (own_rank // bit) % 2
        keep = lax.dynamic_slice_in_dim(rows, side * half, half, axis=0)
        send = lax.dynamic_slice_in_dim(rows, (1 - side) * half, half, axis=0)
        rows = merge_rows(keep, lax.ppermute(send, "tp", partner_pairs(count, bit)))
    return rows


def state_rows(peak, total, weighted):
    row_count = peak.shape[0] * peak.shape[1]
    return jnp.concatenate(
        [weighted.reshape(row_count, -1), total.reshape(row_count, 1), peak.reshape(row_count, 1)],
        axis=1,
    )


def exchange_gather(values):
    count = lax.axis_size("tp")
    copies = jnp.broadcast_to(values[None], (count,) + values.shape)
    received = lax.all_to_all(copies, "tp", 0, 0, tiled=True)
    return jnp.transpose(received, (1, 0, 2)).reshape(values.shape[0], -1)


def exchange_scatter_sum(blocks):
    received = lax.all_to_all(blocks, "tp", 0, 0, tiled=True)
    return jnp.sum(received.astype(jnp.float32), axis=0)


def reverse_blocks(values, count):
    rows, width = values.shape
    levels = count.bit_length() - 1
    split = values.reshape((rows,) + (2,) * levels + (width // count,))
    order = (0,) + tuple(range(levels, 0, -1)) + (levels + 1,)
    return split.transpose(order).reshape(rows, width)


def on_device(
    hidden,
    attn_gain,
    w_qkv,
    w_out,
    prefix_keys,
    prefix_values,
    private_keys,
    private_values,
    group_ids,
    private_lengths,
    moe_gain,
    router,
    w_gate,
    w_up,
    w_down,
    routes,
):
    model_width = w_out.shape[0]
    all_tokens = hidden.shape[0]
    requests = group_ids.shape[0]
    group_count = prefix_keys.shape[0]
    prefix_block = prefix_keys.shape[1]
    private_block = private_keys.shape[1]
    own_rank = lax.axis_index("tp")
    score_scale = HDIM ** (-0.5)
    scaled = (hidden * attn_gain[None, :]).astype(jnp.bfloat16)
    partial_qkv = jnp.dot(scaled, w_qkv, preferred_element_type=jnp.float32)
    own_squares = jnp.sum(hidden * hidden, axis=1)
    qkv_width = partial_qkv.shape[1]
    tp_count = lax.axis_size("tp")
    block = qkv_width // tp_count
    packed = jnp.concatenate(
        [
            partial_qkv.reshape(all_tokens, tp_count, block),
            jnp.broadcast_to(own_squares[:, None, None], (all_tokens, tp_count, 1)),
        ],
        axis=2,
    ).reshape(all_tokens, tp_count * (block + 1))
    _, all_bits = tp_bits()
    near_bits = all_bits[: len(all_bits) // 2]
    far_bits = all_bits[len(all_bits) // 2 :]
    own_block = exchange_sum(scatter_sum(packed, near_bits), far_bits)
    own_block = own_block.reshape(all_tokens, -1, block + 1)
    inv_attn = lax.rsqrt(own_block[:, 0, block] / model_width + EPSILON)
    own_qkv = (inv_attn[:, None, None] * own_block[:, :, :block]).astype(jnp.bfloat16)
    qkv = gather_cols(own_qkv.reshape(all_tokens, -1), bits=near_bits)
    own_lengths = jnp.broadcast_to(private_lengths[:, None], (requests, NEW)).reshape(all_tokens)
    places = (
        prefix_block * lax.axis_size("tp")
        + own_lengths
        + jnp.arange(all_tokens, dtype=jnp.int32) % NEW
    )
    queries = rotate_heads(
        qkv[:, :model_width].astype(jnp.float32).reshape(all_tokens, HEADS, HDIM), places
    ).astype(jnp.bfloat16)
    fresh_keys = rotate_heads(
        qkv[:, model_width : 2 * model_width].astype(jnp.float32).reshape(all_tokens, HEADS, HDIM),
        places,
    ).astype(jnp.bfloat16)
    fresh_values = qkv[:, 2 * model_width :].astype(jnp.float32).reshape(requests, NEW, HEADS, HDIM)
    query_f = queries.astype(jnp.float32).reshape(requests, NEW, HEADS, HDIM)
    pre_keys = prefix_keys.astype(jnp.float32).reshape(group_count, prefix_block, HEADS, HDIM)
    pre_scores = jnp.einsum("rjhd,gphd->rjhgp", query_f, pre_keys) * score_scale
    member = group_ids[:, None] == jnp.arange(group_count, dtype=jnp.int32)[None, :]
    pre_scores = jnp.where(member[:, None, None, :, None], pre_scores, BLOCKED)
    priv_keys = private_keys.astype(jnp.float32).reshape(requests, private_block, HEADS, HDIM)
    priv_scores = jnp.einsum("rjhd,rphd->rjhp", query_f, priv_keys) * score_scale
    slots = own_rank * private_block + jnp.arange(private_block, dtype=jnp.int32)
    live = slots[None, :] < private_lengths[:, None]
    priv_scores = jnp.where(live[:, None, None, :], priv_scores, BLOCKED)
    local_peak = jnp.maximum(jnp.max(pre_scores, axis=(3, 4)), jnp.max(priv_scores, axis=3))
    pre_weights = jnp.exp(pre_scores - local_peak[..., None, None])
    priv_weights = jnp.exp(priv_scores - local_peak[..., None])
    local_total = jnp.sum(pre_weights, axis=(3, 4)) + jnp.sum(priv_weights, axis=3)
    pre_vals = prefix_values.astype(jnp.float32).reshape(group_count, prefix_block, HEADS, HDIM)
    priv_vals = private_values.astype(jnp.float32).reshape(requests, private_block, HEADS, HDIM)
    local_weighted = jnp.einsum("rjhgp,gphd->rjhd", pre_weights, pre_vals) + jnp.einsum(
        "rjhp,rphd->rjhd", priv_weights, priv_vals
    )
    local_peak = local_peak.reshape(all_tokens, HEADS)
    local_total = local_total.reshape(all_tokens, HEADS)
    local_weighted = local_weighted.reshape(all_tokens, model_width)
    cache_rows = scatter_merge(state_rows(local_peak, local_total, local_weighted), near_bits)
    cache_rows = exchange_merge(cache_rows, far_bits)
    key_f = fresh_keys.astype(jnp.float32).reshape(requests, NEW, HEADS, HDIM)
    new_scores = jnp.einsum("rjhd,rihd->rjhi", query_f, key_f) * score_scale
    causal = jnp.arange(NEW)[:, None] >= jnp.arange(NEW)[None, :]
    new_scores = jnp.where(causal[None, :, None, :], new_scores, BLOCKED)
    new_peak = jnp.max(new_scores, axis=3)
    new_weights = jnp.exp(new_scores - new_peak[..., None])
    new_total = jnp.sum(new_weights, axis=3).reshape(all_tokens, HEADS)
    new_weighted = jnp.einsum("rjhi,rihd->rjhd", new_weights, fresh_values).reshape(
        all_tokens, model_width
    )
    new_peak = new_peak.reshape(all_tokens, HEADS)
    new_rows = state_rows(new_peak, new_total, new_weighted)
    own_count = cache_rows.shape[0]
    new_rows = lax.dynamic_slice_in_dim(new_rows, kept_position(near_bits) * own_count, own_count, axis=0)
    final_rows = merge_rows(cache_rows, new_rows)
    attended_rows = (final_rows[:, :HDIM] / final_rows[:, HDIM : HDIM + 1]).astype(jnp.bfloat16)
    attended_lines = attended_rows.reshape(attended_rows.shape[0] // 2, 2 * HDIM)
    attended = gather_cols(attended_lines, axis=0, bits=near_bits).reshape(all_tokens, model_width)
    residual_cols = hidden + jnp.dot(attended, w_out, preferred_element_type=jnp.float32)
    full_rows = exchange_gather(residual_cols.astype(jnp.bfloat16)).astype(jnp.float32)
    inv_norm = lax.rsqrt(jnp.mean(full_rows * full_rows, axis=1) + EPSILON)
    normed = (full_rows * inv_norm[:, None] * moe_gain[None, :]).astype(jnp.bfloat16)
    logits = jnp.dot(normed, router, preferred_element_type=jnp.float32)
    expert_ids = jnp.arange(logits.shape[1], dtype=jnp.int32)
    first_pick = routes[:, 0:1] == expert_ids[None, :]
    second_pick = routes[:, 1:2] == expert_ids[None, :]
    first_logit = jnp.sum(jnp.where(first_pick, logits, 0.0), axis=1)
    second_logit = jnp.sum(jnp.where(second_pick, logits, 0.0), axis=1)
    first_weight = jax.nn.sigmoid(first_logit - second_logit)
    unit_count = w_gate.shape[1]
    own_expert = own_rank * unit_count // FF
    mix_coef = first_weight * (routes[:, 0] == own_expert).astype(jnp.float32) + (
        1.0 - first_weight
    ) * (routes[:, 1] == own_expert).astype(jnp.float32)
    gate_out = jnp.dot(normed, w_gate, preferred_element_type=jnp.float32)
    up_out = jnp.dot(normed, w_up, preferred_element_type=jnp.float32)
    inner_act = (jax.nn.silu(gate_out) * up_out * mix_coef[:, None]).astype(jnp.bfloat16)
    expert_blocks = jnp.einsum(
        "tf,fbc->btc",
        inner_act,
        w_down.reshape(w_down.shape[0], tp_count, -1),
        preferred_element_type=jnp.float32,
    )
    return residual_cols + exchange_scatter_sum(expert_blocks.astype(jnp.bfloat16))


def solution(mesh):
    placed = (
        P("rep", "tp"),
        P("tp"),
        P("tp", None),
        P(None, "tp"),
        P("rep", "tp", None),
        P("rep", "tp", None),
        P("rep", "tp", None),
        P("rep", "tp", None),
        P("rep"),
        P("rep"),
        P(),
        P(),
        P(None, "tp"),
        P(None, "tp"),
        P("tp", None),
        P("rep", None),
    )
    return jax.shard_map(
        on_device, mesh=mesh, in_specs=placed, out_specs=P("rep", "tp"), check_vma=False
    )
```

```python
import jax
import jax.numpy as jnp
from jax import lax
from jax.sharding import PartitionSpec as P

HEADS = 36
HDIM = 64
FF = 2880
NEW = 4


EPSILON = 1e-05
BLOCKED = -1e30


def rotate_heads(vectors, places):
    half_dim = HDIM // 2
    frequencies = 10000.0 ** (-jnp.arange(half_dim, dtype=jnp.float32) / half_dim)
    angles = places.astype(jnp.float32)[:, None] * frequencies[None, :]
    cosine = jnp.cos(angles)[:, None, :]
    sine_part = jnp.sin(angles)[:, None, :]
    first = vectors[..., :half_dim]
    second = vectors[..., half_dim:]
    return jnp.concatenate(
        [first * cosine - second * sine_part, second * cosine + first * sine_part], axis=-1
    )


def scale_rows(values, factor):
    row_count, head_count = factor.shape
    return (values.reshape(row_count, head_count, -1) * factor[..., None]).reshape(row_count, -1)


def partner_pairs(count, bit):
    return [(i, i ^ bit) for i in range(count)]


def tp_bits():
    count = lax.axis_size("tp")
    bits = []
    bit = 1
    while bit < count:
        bits.append(bit)
        bit *= 2
    return count, bits


def scatter_sum(values, bits=None):
    count, all_bits = tp_bits()
    bits = all_bits if bits is None else bits
    own_rank = lax.axis_index("tp")
    for bit in bits:
        half = values.shape[1] // 2
        side = (own_rank // bit) % 2
        keep = lax.dynamic_slice_in_dim(values, side * half, half, axis=1)
        send = lax.dynamic_slice_in_dim(values, (1 - side) * half, half, axis=1)
        values = keep + lax.ppermute(send, "tp", partner_pairs(count, bit))
    return values


def gather_cols(values, axis=1, bits=None):
    count, all_bits = tp_bits()
    bits = all_bits if bits is None else bits
    own_rank = lax.axis_index("tp")
    for bit in reversed(bits):
        side = (own_rank // bit) % 2
        other = lax.ppermute(values, "tp", partner_pairs(count, bit))
        values = jnp.where(
            side == 0,
            jnp.concatenate([values, other], axis=axis),
            jnp.concatenate([other, values], axis=axis),
        )
    return values


def kept_position(bits):
    own_rank = lax.axis_index("tp")
    position = 0
    for level, bit in enumerate(bits):
        position = position + ((own_rank // bit) % 2) * 2 ** (len(bits) - 1 - level)
    return position


def exchange_sum(values, bits):
    count, _ = tp_bits()
    for bit in bits:
        values = values + lax.ppermute(values, "tp", partner_pairs(count, bit))
    return values


def exchange_merge(rows, bits):
    count, _ = tp_bits()
    for bit in bits:
        rows = merge_rows(rows, lax.ppermute(rows, "tp", partner_pairs(count, bit)))
    return rows


def merge_rows(first, second):
    joint = jnp.maximum(first[:, -1:], second[:, -1:])
    first_factor = jnp.exp(first[:, -1:] - joint)
    second_factor = jnp.exp(second[:, -1:] - joint)
    body = first[:, :-1] * first_factor + second[:, :-1] * second_factor
    return jnp.concatenate([body, joint], axis=1)


def scatter_merge(rows, bits):
    count, _ = tp_bits()
    own_rank = lax.axis_index("tp")
    for bit in bits:
        half = rows.shape[0] // 2
        side = (own_rank // bit) % 2
        keep = lax.dynamic_slice_in_dim(rows, side * half, half, axis=0)
        send = lax.dynamic_slice_in_dim(rows, (1 - side) * half, half, axis=0)
        rows = merge_rows(keep, lax.ppermute(send, "tp", partner_pairs(count, bit)))
    return rows


def state_rows(peak, total, weighted):
    row_count = peak.shape[0] * peak.shape[1]
    return jnp.concatenate(
        [weighted.reshape(row_count, -1), total.reshape(row_count, 1), peak.reshape(row_count, 1)],
        axis=1,
    )


def exchange_gather(values):
    count = lax.axis_size("tp")
    copies = jnp.broadcast_to(values[None], (count,) + values.shape)
    received = lax.all_to_all(copies, "tp", 0, 0, tiled=True)
    return jnp.transpose(received, (1, 0, 2)).reshape(values.shape[0], -1)


def exchange_scatter_sum(blocks):
    received = lax.all_to_all(blocks, "tp", 0, 0, tiled=True)
    return jnp.sum(received.astype(jnp.float32), axis=0)


def reverse_blocks(values, count):
    rows, width = values.shape
    levels = count.bit_length() - 1
    split = values.reshape((rows,) + (2,) * levels + (width // count,))
    order = (0,) + tuple(range(levels, 0, -1)) + (levels + 1,)
    return split.transpose(order).reshape(rows, width)


def on_device(
    hidden,
    attn_gain,
    w_qkv,
    w_out,
    prefix_keys,
    prefix_values,
    private_keys,
    private_values,
    group_ids,
    private_lengths,
    moe_gain,
    router,
    w_gate,
    w_up,
    w_down,
    routes,
):
    model_width = w_out.shape[0]
    all_tokens = hidden.shape[0]
    requests = group_ids.shape[0]
    group_count = prefix_keys.shape[0]
    prefix_block = prefix_keys.shape[1]
    private_block = private_keys.shape[1]
    own_rank = lax.axis_index("tp")
    score_scale = HDIM ** (-0.5)
    scaled = (hidden * attn_gain[None, :]).astype(jnp.bfloat16)
    partial_qkv = jnp.dot(scaled, w_qkv, preferred_element_type=jnp.float32)
    own_squares = jnp.sum(hidden * hidden, axis=1)
    qkv_width = partial_qkv.shape[1]
    tp_count = lax.axis_size("tp")
    block = qkv_width // tp_count
    packed = jnp.concatenate(
        [
            partial_qkv.reshape(all_tokens, tp_count, block),
            jnp.broadcast_to(own_squares[:, None, None], (all_tokens, tp_count, 1)),
        ],
        axis=2,
    ).reshape(all_tokens, tp_count * (block + 1))
    _, all_bits = tp_bits()
    near_bits = all_bits[: len(all_bits) // 2]
    far_bits = all_bits[len(all_bits) // 2 :]
    own_block = exchange_sum(scatter_sum(packed, near_bits), far_bits)
    own_block = own_block.reshape(all_tokens, -1, block + 1)
    inv_attn = lax.rsqrt(own_block[:, 0, block] / model_width + EPSILON)
    own_qkv = (inv_attn[:, None, None] * own_block[:, :, :block]).astype(jnp.bfloat16)
    qkv = gather_cols(own_qkv.reshape(all_tokens, -1), bits=near_bits)
    own_lengths = jnp.broadcast_to(private_lengths[:, None], (requests, NEW)).reshape(all_tokens)
    places = (
        prefix_block * lax.axis_size("tp")
        + own_lengths
        + jnp.arange(all_tokens, dtype=jnp.int32) % NEW
    )
    queries = rotate_heads(
        qkv[:, :model_width].astype(jnp.float32).reshape(all_tokens, HEADS, HDIM), places
    ).astype(jnp.bfloat16)
    fresh_keys = rotate_heads(
        qkv[:, model_width : 2 * model_width].astype(jnp.float32).reshape(all_tokens, HEADS, HDIM),
        places,
    ).astype(jnp.bfloat16)
    fresh_values = qkv[:, 2 * model_width :].astype(jnp.float32).reshape(requests, NEW, HEADS, HDIM)
    query_f = queries.astype(jnp.float32).reshape(requests, NEW, HEADS, HDIM)
    query_b = queries.reshape(requests, NEW, HEADS, HDIM)
    pre_keys = prefix_keys.reshape(group_count, prefix_block, HEADS, HDIM)
    pre_scores = (
        jnp.einsum("rjhd,gphd->rjhgp", query_b, pre_keys, preferred_element_type=jnp.float32)
        * score_scale
    )
    member = group_ids[:, None] == jnp.arange(group_count, dtype=jnp.int32)[None, :]
    pre_scores = jnp.where(member[:, None, None, :, None], pre_scores, BLOCKED)
    priv_keys = private_keys.reshape(requests, private_block, HEADS, HDIM)
    priv_scores = (
        jnp.einsum("rjhd,rphd->rjhp", query_b, priv_keys, preferred_element_type=jnp.float32)
        * score_scale
    )
    slots = own_rank * private_block + jnp.arange(private_block, dtype=jnp.int32)
    live = slots[None, :] < private_lengths[:, None]
    priv_scores = jnp.where(live[:, None, None, :], priv_scores, BLOCKED)
    local_peak = jnp.maximum(jnp.max(pre_scores, axis=(3, 4)), jnp.max(priv_scores, axis=3))
    pre_weights = jnp.exp(pre_scores - local_peak[..., None, None])
    priv_weights = jnp.exp(priv_scores - local_peak[..., None])
    local_total = jnp.sum(pre_weights, axis=(3, 4)) + jnp.sum(priv_weights, axis=3)
    pre_vals = prefix_values.astype(jnp.float32).reshape(group_count, prefix_block, HEADS, HDIM)
    priv_vals = private_values.astype(jnp.float32).reshape(requests, private_block, HEADS, HDIM)
    local_weighted = jnp.einsum("rjhgp,gphd->rjhd", pre_weights, pre_vals) + jnp.einsum(
        "rjhp,rphd->rjhd", priv_weights, priv_vals
    )
    local_peak = local_peak.reshape(all_tokens, HEADS)
    local_total = local_total.reshape(all_tokens, HEADS)
    local_weighted = local_weighted.reshape(all_tokens, model_width)
    cache_rows = scatter_merge(state_rows(local_peak, local_total, local_weighted), near_bits)
    cache_rows = exchange_merge(cache_rows, far_bits)
    key_f = fresh_keys.astype(jnp.float32).reshape(requests, NEW, HEADS, HDIM)
    new_scores = jnp.einsum("rjhd,rihd->rjhi", query_f, key_f) * score_scale
    causal = jnp.arange(NEW)[:, None] >= jnp.arange(NEW)[None, :]
    new_scores = jnp.where(causal[None, :, None, :], new_scores, BLOCKED)
    new_peak = jnp.max(new_scores, axis=3)
    new_weights = jnp.exp(new_scores - new_peak[..., None])
    new_total = jnp.sum(new_weights, axis=3).reshape(all_tokens, HEADS)
    new_weighted = jnp.einsum("rjhi,rihd->rjhd", new_weights, fresh_values).reshape(
        all_tokens, model_width
    )
    new_peak = new_peak.reshape(all_tokens, HEADS)
    new_rows = state_rows(new_peak, new_total, new_weighted)
    own_count = cache_rows.shape[0]
    new_rows = lax.dynamic_slice_in_dim(new_rows, kept_position(near_bits) * own_count, own_count, axis=0)
    final_rows = merge_rows(cache_rows, new_rows)
    attended_rows = (final_rows[:, :HDIM] / final_rows[:, HDIM : HDIM + 1]).astype(jnp.bfloat16)
    attended_lines = attended_rows.reshape(attended_rows.shape[0] // 2, 2 * HDIM)
    attended = gather_cols(attended_lines, axis=0, bits=near_bits).reshape(all_tokens, model_width)
    residual_cols = hidden + jnp.dot(attended, w_out, preferred_element_type=jnp.float32)
    full_rows = exchange_gather(residual_cols.astype(jnp.bfloat16)).astype(jnp.float32)
    inv_norm = lax.rsqrt(jnp.mean(full_rows * full_rows, axis=1) + EPSILON)
    normed = (full_rows * inv_norm[:, None] * moe_gain[None, :]).astype(jnp.bfloat16)
    logits = jnp.dot(normed, router, preferred_element_type=jnp.float32)
    expert_ids = jnp.arange(logits.shape[1], dtype=jnp.int32)
    first_pick = routes[:, 0:1] == expert_ids[None, :]
    second_pick = routes[:, 1:2] == expert_ids[None, :]
    first_logit = jnp.sum(jnp.where(first_pick, logits, 0.0), axis=1)
    second_logit = jnp.sum(jnp.where(second_pick, logits, 0.0), axis=1)
    first_weight = jax.nn.sigmoid(first_logit - second_logit)
    unit_count = w_gate.shape[1]
    own_expert = own_rank * unit_count // FF
    mix_coef = first_weight * (routes[:, 0] == own_expert).astype(jnp.float32) + (
        1.0 - first_weight
    ) * (routes[:, 1] == own_expert).astype(jnp.float32)
    gate_out = jnp.dot(normed, w_gate, preferred_element_type=jnp.float32)
    up_out = jnp.dot(normed, w_up, preferred_element_type=jnp.float32)
    inner_act = (jax.nn.silu(gate_out) * up_out * mix_coef[:, None]).astype(jnp.bfloat16)
    expert_blocks = jnp.einsum(
        "tf,fbc->btc",
        inner_act,
        w_down.reshape(w_down.shape[0], tp_count, -1),
        preferred_element_type=jnp.float32,
    )
    return residual_cols + exchange_scatter_sum(expert_blocks.astype(jnp.bfloat16))


def solution(mesh):
    placed = (
        P("rep", "tp"),
        P("tp"),
        P("tp", None),
        P(None, "tp"),
        P("rep", "tp", None),
        P("rep", "tp", None),
        P("rep", "tp", None),
        P("rep", "tp", None),
        P("rep"),
        P("rep"),
        P(),
        P(),
        P(None, "tp"),
        P(None, "tp"),
        P("tp", None),
        P("rep", None),
    )
    return jax.shard_map(
        on_device, mesh=mesh, in_specs=placed, out_specs=P("rep", "tp"), check_vma=False
    )
```

```python
import jax
import jax.numpy as jnp
from jax import lax
from jax.sharding import PartitionSpec as P

HEADS = 36
HDIM = 64
FF = 2880
NEW = 4


EPSILON = 1e-05
BLOCKED = -1e30


def rotate_heads(vectors, places):
    half_dim = HDIM // 2
    frequencies = 10000.0 ** (-jnp.arange(half_dim, dtype=jnp.float32) / half_dim)
    angles = places.astype(jnp.float32)[:, None] * frequencies[None, :]
    cosine = jnp.cos(angles)[:, None, :]
    sine_part = jnp.sin(angles)[:, None, :]
    first = vectors[..., :half_dim]
    second = vectors[..., half_dim:]
    return jnp.concatenate(
        [first * cosine - second * sine_part, second * cosine + first * sine_part], axis=-1
    )


def scale_rows(values, factor):
    row_count, head_count = factor.shape
    return (values.reshape(row_count, head_count, -1) * factor[..., None]).reshape(row_count, -1)


def partner_pairs(count, bit):
    return [(i, i ^ bit) for i in range(count)]


def tp_bits():
    count = lax.axis_size("tp")
    bits = []
    bit = 1
    while bit < count:
        bits.append(bit)
        bit *= 2
    return count, bits


def scatter_sum(values, bits=None):
    count, all_bits = tp_bits()
    bits = all_bits if bits is None else bits
    own_rank = lax.axis_index("tp")
    for bit in bits:
        half = values.shape[1] // 2
        side = (own_rank // bit) % 2
        keep = lax.dynamic_slice_in_dim(values, side * half, half, axis=1)
        send = lax.dynamic_slice_in_dim(values, (1 - side) * half, half, axis=1)
        values = keep + lax.ppermute(send, "tp", partner_pairs(count, bit))
    return values


def gather_cols(values, axis=1, bits=None):
    count, all_bits = tp_bits()
    bits = all_bits if bits is None else bits
    own_rank = lax.axis_index("tp")
    for bit in reversed(bits):
        side = (own_rank // bit) % 2
        other = lax.ppermute(values, "tp", partner_pairs(count, bit))
        values = jnp.where(
            side == 0,
            jnp.concatenate([values, other], axis=axis),
            jnp.concatenate([other, values], axis=axis),
        )
    return values


def kept_position(bits):
    own_rank = lax.axis_index("tp")
    position = 0
    for level, bit in enumerate(bits):
        position = position + ((own_rank // bit) % 2) * 2 ** (len(bits) - 1 - level)
    return position


def exchange_sum(values, bits):
    count, _ = tp_bits()
    for bit in bits:
        values = values + lax.ppermute(values, "tp", partner_pairs(count, bit))
    return values


def exchange_merge(rows, bits):
    count, _ = tp_bits()
    for bit in bits:
        rows = merge_rows(rows, lax.ppermute(rows, "tp", partner_pairs(count, bit)))
    return rows


def merge_rows(first, second):
    joint = jnp.maximum(first[:, -1:], second[:, -1:])
    first_factor = jnp.exp(first[:, -1:] - joint)
    second_factor = jnp.exp(second[:, -1:] - joint)
    body = first[:, :-1] * first_factor + second[:, :-1] * second_factor
    return jnp.concatenate([body, joint], axis=1)


def scatter_merge(rows, bits):
    count, _ = tp_bits()
    own_rank = lax.axis_index("tp")
    for bit in bits:
        half = rows.shape[0] // 2
        side = (own_rank // bit) % 2
        keep = lax.dynamic_slice_in_dim(rows, side * half, half, axis=0)
        send = lax.dynamic_slice_in_dim(rows, (1 - side) * half, half, axis=0)
        rows = merge_rows(keep, lax.ppermute(send, "tp", partner_pairs(count, bit)))
    return rows


def state_rows(peak, total, weighted):
    row_count = peak.shape[0] * peak.shape[1]
    return jnp.concatenate(
        [weighted.reshape(row_count, -1), total.reshape(row_count, 1), peak.reshape(row_count, 1)],
        axis=1,
    )


def exchange_gather(values):
    count = lax.axis_size("tp")
    copies = jnp.broadcast_to(values[None], (count,) + values.shape)
    received = lax.all_to_all(copies, "tp", 0, 0, tiled=True)
    return jnp.transpose(received, (1, 0, 2)).reshape(values.shape[0], -1)


def exchange_scatter_sum(blocks):
    received = lax.all_to_all(blocks, "tp", 0, 0, tiled=True)
    return jnp.sum(received.astype(jnp.float32), axis=0)


def merge_states(first, second, heads):
    width = first.shape[1] - 2 * heads
    joint = jnp.maximum(first[:, width + heads :], second[:, width + heads :])
    first_factor = jnp.exp(first[:, width + heads :] - joint)
    second_factor = jnp.exp(second[:, width + heads :] - joint)
    total = first[:, width : width + heads] * first_factor + second[:, width : width + heads] * second_factor
    weighted = scale_rows(first[:, :width], first_factor) + scale_rows(second[:, :width], second_factor)
    return jnp.concatenate([weighted, total, joint], axis=1)


def scatter_states(states, bits, heads):
    count, _ = tp_bits()
    own_rank = lax.axis_index("tp")
    for bit in bits:
        half = states.shape[0] // 2
        side = (own_rank // bit) % 2
        keep = lax.dynamic_slice_in_dim(states, side * half, half, axis=0)
        send = lax.dynamic_slice_in_dim(states, (1 - side) * half, half, axis=0)
        states = merge_states(keep, lax.ppermute(send, "tp", partner_pairs(count, bit)), heads)
    return states


def exchange_states(states, bits, heads):
    count, _ = tp_bits()
    for bit in bits:
        states = merge_states(states, lax.ppermute(states, "tp", partner_pairs(count, bit)), heads)
    return states


def reverse_blocks(values, count):
    rows, width = values.shape
    levels = count.bit_length() - 1
    split = values.reshape((rows,) + (2,) * levels + (width // count,))
    order = (0,) + tuple(range(levels, 0, -1)) + (levels + 1,)
    return split.transpose(order).reshape(rows, width)


def on_device(
    hidden,
    attn_gain,
    w_qkv,
    w_out,
    prefix_keys,
    prefix_values,
    private_keys,
    private_values,
    group_ids,
    private_lengths,
    moe_gain,
    router,
    w_gate,
    w_up,
    w_down,
    routes,
):
    model_width = w_out.shape[0]
    all_tokens = hidden.shape[0]
    requests = group_ids.shape[0]
    group_count = prefix_keys.shape[0]
    prefix_block = prefix_keys.shape[1]
    private_block = private_keys.shape[1]
    own_rank = lax.axis_index("tp")
    score_scale = HDIM ** (-0.5)
    scaled = (hidden * attn_gain[None, :]).astype(jnp.bfloat16)
    partial_qkv = jnp.dot(scaled, w_qkv, preferred_element_type=jnp.float32)
    own_squares = jnp.sum(hidden * hidden, axis=1)
    qkv_width = partial_qkv.shape[1]
    tp_count = lax.axis_size("tp")
    block = qkv_width // tp_count
    packed = jnp.concatenate(
        [
            partial_qkv.reshape(all_tokens, tp_count, block),
            jnp.broadcast_to(own_squares[:, None, None], (all_tokens, tp_count, 1)),
        ],
        axis=2,
    ).reshape(all_tokens, tp_count * (block + 1))
    _, all_bits = tp_bits()
    near_bits = all_bits[: len(all_bits) // 2]
    far_bits = all_bits[len(all_bits) // 2 :]
    own_block = exchange_sum(scatter_sum(packed, near_bits), far_bits)
    own_block = own_block.reshape(all_tokens, -1, block + 1)
    inv_attn = lax.rsqrt(own_block[:, 0, block] / model_width + EPSILON)
    own_qkv = (inv_attn[:, None, None] * own_block[:, :, :block]).astype(jnp.bfloat16)
    qkv = gather_cols(own_qkv.reshape(all_tokens, -1), bits=near_bits)
    own_lengths = jnp.broadcast_to(private_lengths[:, None], (requests, NEW)).reshape(all_tokens)
    places = (
        prefix_block * lax.axis_size("tp")
        + own_lengths
        + jnp.arange(all_tokens, dtype=jnp.int32) % NEW
    )
    queries = rotate_heads(
        qkv[:, :model_width].astype(jnp.float32).reshape(all_tokens, HEADS, HDIM), places
    ).astype(jnp.bfloat16)
    fresh_keys = rotate_heads(
        qkv[:, model_width : 2 * model_width].astype(jnp.float32).reshape(all_tokens, HEADS, HDIM),
        places,
    ).astype(jnp.bfloat16)
    fresh_values = qkv[:, 2 * model_width :].astype(jnp.float32).reshape(requests, NEW, HEADS, HDIM)
    query_f = queries.astype(jnp.float32).reshape(requests, NEW, HEADS, HDIM)
    query_b = queries.reshape(requests, NEW, HEADS, HDIM)
    pre_keys = prefix_keys.reshape(group_count, prefix_block, HEADS, HDIM)
    pre_scores = (
        jnp.einsum("rjhd,gphd->rjhgp", query_b, pre_keys, preferred_element_type=jnp.float32)
        * score_scale
    )
    member = group_ids[:, None] == jnp.arange(group_count, dtype=jnp.int32)[None, :]
    pre_scores = jnp.where(member[:, None, None, :, None], pre_scores, BLOCKED)
    priv_keys = private_keys.reshape(requests, private_block, HEADS, HDIM)
    priv_scores = (
        jnp.einsum("rjhd,rphd->rjhp", query_b, priv_keys, preferred_element_type=jnp.float32)
        * score_scale
    )
    slots = own_rank * private_block + jnp.arange(private_block, dtype=jnp.int32)
    live = slots[None, :] < private_lengths[:, None]
    priv_scores = jnp.where(live[:, None, None, :], priv_scores, BLOCKED)
    local_peak = jnp.maximum(jnp.max(pre_scores, axis=(3, 4)), jnp.max(priv_scores, axis=3))
    pre_weights = jnp.exp(pre_scores - local_peak[..., None, None])
    priv_weights = jnp.exp(priv_scores - local_peak[..., None])
    local_total = jnp.sum(pre_weights, axis=(3, 4)) + jnp.sum(priv_weights, axis=3)
    pre_vals = prefix_values.astype(jnp.float32).reshape(group_count, prefix_block, HEADS, HDIM)
    priv_vals = private_values.astype(jnp.float32).reshape(requests, private_block, HEADS, HDIM)
    local_weighted = jnp.einsum("rjhgp,gphd->rjhd", pre_weights, pre_vals) + jnp.einsum(
        "rjhp,rphd->rjhd", priv_weights, priv_vals
    )
    local_peak = local_peak.reshape(all_tokens, HEADS)
    local_total = local_total.reshape(all_tokens, HEADS)
    local_weighted = local_weighted.reshape(all_tokens, model_width)
    cache_state = scatter_states(
        jnp.concatenate([local_weighted, local_total, local_peak], axis=1), near_bits, HEADS
    )
    cache_state = exchange_states(cache_state, far_bits, HEADS)
    key_f = fresh_keys.astype(jnp.float32).reshape(requests, NEW, HEADS, HDIM)
    new_scores = jnp.einsum("rjhd,rihd->rjhi", query_f, key_f) * score_scale
    causal = jnp.arange(NEW)[:, None] >= jnp.arange(NEW)[None, :]
    new_scores = jnp.where(causal[None, :, None, :], new_scores, BLOCKED)
    new_peak = jnp.max(new_scores, axis=3)
    new_weights = jnp.exp(new_scores - new_peak[..., None])
    new_total = jnp.sum(new_weights, axis=3).reshape(all_tokens, HEADS)
    new_weighted = jnp.einsum("rjhi,rihd->rjhd", new_weights, fresh_values).reshape(
        all_tokens, model_width
    )
    new_peak = new_peak.reshape(all_tokens, HEADS)
    new_state = jnp.concatenate([new_weighted, new_total, new_peak], axis=1)
    own_count = cache_state.shape[0]
    new_state = lax.dynamic_slice_in_dim(new_state, kept_position(near_bits) * own_count, own_count, axis=0)
    final_state = merge_states(cache_state, new_state, HEADS)
    final_weighted = final_state[:, :model_width].reshape(own_count, HEADS, HDIM)
    final_total = final_state[:, model_width : model_width + HEADS]
    attended_own = (final_weighted / final_total[..., None]).astype(jnp.bfloat16)
    attended_lines = attended_own.reshape(own_count * HEADS // 2, 2 * HDIM)
    attended = gather_cols(attended_lines, axis=0, bits=near_bits).reshape(all_tokens, model_width)
    residual_cols = hidden + jnp.dot(attended, w_out, preferred_element_type=jnp.float32)
    full_rows = exchange_gather(residual_cols.astype(jnp.bfloat16)).astype(jnp.float32)
    inv_norm = lax.rsqrt(jnp.mean(full_rows * full_rows, axis=1) + EPSILON)
    normed = (full_rows * inv_norm[:, None] * moe_gain[None, :]).astype(jnp.bfloat16)
    logits = jnp.dot(normed, router, preferred_element_type=jnp.float32)
    expert_ids = jnp.arange(logits.shape[1], dtype=jnp.int32)
    first_pick = routes[:, 0:1] == expert_ids[None, :]
    second_pick = routes[:, 1:2] == expert_ids[None, :]
    first_logit = jnp.sum(jnp.where(first_pick, logits, 0.0), axis=1)
    second_logit = jnp.sum(jnp.where(second_pick, logits, 0.0), axis=1)
    first_weight = jax.nn.sigmoid(first_logit - second_logit)
    unit_count = w_gate.shape[1]
    own_expert = own_rank * unit_count // FF
    mix_coef = first_weight * (routes[:, 0] == own_expert).astype(jnp.float32) + (
        1.0 - first_weight
    ) * (routes[:, 1] == own_expert).astype(jnp.float32)
    gate_out = jnp.dot(normed, w_gate, preferred_element_type=jnp.float32)
    up_out = jnp.dot(normed, w_up, preferred_element_type=jnp.float32)
    inner_act = (jax.nn.silu(gate_out) * up_out * mix_coef[:, None]).astype(jnp.bfloat16)
    expert_blocks = jnp.einsum(
        "tf,fbc->btc",
        inner_act,
        w_down.reshape(w_down.shape[0], tp_count, -1),
        preferred_element_type=jnp.float32,
    )
    return residual_cols + exchange_scatter_sum(expert_blocks.astype(jnp.bfloat16))


def solution(mesh):
    placed = (
        P("rep", "tp"),
        P("tp"),
        P("tp", None),
        P(None, "tp"),
        P("rep", "tp", None),
        P("rep", "tp", None),
        P("rep", "tp", None),
        P("rep", "tp", None),
        P("rep"),
        P("rep"),
        P(),
        P(),
        P(None, "tp"),
        P(None, "tp"),
        P("tp", None),
        P("rep", None),
    )
    return jax.shard_map(
        on_device, mesh=mesh, in_specs=placed, out_specs=P("rep", "tp"), check_vma=False
    )
```

```python
import jax
import jax.numpy as jnp
from jax import lax
from jax.sharding import PartitionSpec as P

HEADS = 36
HDIM = 64
FF = 2880
NEW = 4


EPSILON = 1e-05
BLOCKED = -1e30


def rotate_heads(vectors, places):
    half_dim = HDIM // 2
    frequencies = 10000.0 ** (-jnp.arange(half_dim, dtype=jnp.float32) / half_dim)
    angles = places.astype(jnp.float32)[:, None] * frequencies[None, :]
    cosine = jnp.cos(angles)[:, None, :]
    sine_part = jnp.sin(angles)[:, None, :]
    first = vectors[..., :half_dim]
    second = vectors[..., half_dim:]
    return jnp.concatenate(
        [first * cosine - second * sine_part, second * cosine + first * sine_part], axis=-1
    )


def scale_rows(values, factor):
    row_count, head_count = factor.shape
    return (values.reshape(row_count, head_count, -1) * factor[..., None]).reshape(row_count, -1)


def partner_pairs(count, bit):
    return [(i, i ^ bit) for i in range(count)]


def tp_bits():
    count = lax.axis_size("tp")
    bits = []
    bit = 1
    while bit < count:
        bits.append(bit)
        bit *= 2
    return count, bits


def scatter_sum(values, bits=None):
    count, all_bits = tp_bits()
    bits = all_bits if bits is None else bits
    own_rank = lax.axis_index("tp")
    for bit in bits:
        half = values.shape[1] // 2
        side = (own_rank // bit) % 2
        keep = lax.dynamic_slice_in_dim(values, side * half, half, axis=1)
        send = lax.dynamic_slice_in_dim(values, (1 - side) * half, half, axis=1)
        values = keep + lax.ppermute(send, "tp", partner_pairs(count, bit))
    return values


def gather_cols(values, axis=1, bits=None):
    count, all_bits = tp_bits()
    bits = all_bits if bits is None else bits
    own_rank = lax.axis_index("tp")
    for bit in reversed(bits):
        side = (own_rank // bit) % 2
        other = lax.ppermute(values, "tp", partner_pairs(count, bit))
        values = jnp.where(
            side == 0,
            jnp.concatenate([values, other], axis=axis),
            jnp.concatenate([other, values], axis=axis),
        )
    return values


def kept_position(bits):
    own_rank = lax.axis_index("tp")
    position = 0
    for level, bit in enumerate(bits):
        position = position + ((own_rank // bit) % 2) * 2 ** (len(bits) - 1 - level)
    return position


def exchange_sum(values, bits):
    count, _ = tp_bits()
    for bit in bits:
        values = values + lax.ppermute(values, "tp", partner_pairs(count, bit))
    return values


def exchange_merge(rows, bits):
    count, _ = tp_bits()
    for bit in bits:
        rows = merge_rows(rows, lax.ppermute(rows, "tp", partner_pairs(count, bit)))
    return rows


def merge_rows(first, second):
    joint = jnp.maximum(first[:, -1:], second[:, -1:])
    first_factor = jnp.exp(first[:, -1:] - joint)
    second_factor = jnp.exp(second[:, -1:] - joint)
    body = first[:, :-1] * first_factor + second[:, :-1] * second_factor
    return jnp.concatenate([body, joint], axis=1)


def scatter_merge(rows, bits):
    count, _ = tp_bits()
    own_rank = lax.axis_index("tp")
    for bit in bits:
        half = rows.shape[0] // 2
        side = (own_rank // bit) % 2
        keep = lax.dynamic_slice_in_dim(rows, side * half, half, axis=0)
        send = lax.dynamic_slice_in_dim(rows, (1 - side) * half, half, axis=0)
        rows = merge_rows(keep, lax.ppermute(send, "tp", partner_pairs(count, bit)))
    return rows


def state_rows(peak, total, weighted):
    row_count = peak.shape[0] * peak.shape[1]
    return jnp.concatenate(
        [weighted.reshape(row_count, -1), total.reshape(row_count, 1), peak.reshape(row_count, 1)],
        axis=1,
    )


def exchange_gather(values):
    count = lax.axis_size("tp")
    copies = jnp.broadcast_to(values[None], (count,) + values.shape)
    received = lax.all_to_all(copies, "tp", 0, 0, tiled=True)
    return jnp.transpose(received, (1, 0, 2)).reshape(values.shape[0], -1)


def exchange_scatter_sum(blocks):
    received = lax.all_to_all(blocks, "tp", 0, 0, tiled=True)
    return jnp.sum(received.astype(jnp.float32), axis=0)


def reverse_blocks(values, count):
    rows, width = values.shape
    levels = count.bit_length() - 1
    split = values.reshape((rows,) + (2,) * levels + (width // count,))
    order = (0,) + tuple(range(levels, 0, -1)) + (levels + 1,)
    return split.transpose(order).reshape(rows, width)


def on_device(
    hidden,
    attn_gain,
    w_qkv,
    w_out,
    prefix_keys,
    prefix_values,
    private_keys,
    private_values,
    group_ids,
    private_lengths,
    moe_gain,
    router,
    w_gate,
    w_up,
    w_down,
    routes,
):
    model_width = w_out.shape[0]
    all_tokens = hidden.shape[0]
    requests = group_ids.shape[0]
    group_count = prefix_keys.shape[0]
    prefix_block = prefix_keys.shape[1]
    private_block = private_keys.shape[1]
    own_rank = lax.axis_index("tp")
    score_scale = HDIM ** (-0.5)
    scaled = (hidden * attn_gain[None, :]).astype(jnp.bfloat16)
    partial_qkv = jnp.dot(scaled, w_qkv, preferred_element_type=jnp.float32)
    own_squares = jnp.sum(hidden * hidden, axis=1)
    qkv_width = partial_qkv.shape[1]
    tp_count = lax.axis_size("tp")
    block = qkv_width // tp_count
    packed = jnp.concatenate(
        [
            partial_qkv.reshape(all_tokens, tp_count, block),
            jnp.broadcast_to(own_squares[:, None, None], (all_tokens, tp_count, 1)),
        ],
        axis=2,
    ).reshape(all_tokens, tp_count * (block + 1))
    _, all_bits = tp_bits()
    near_bits = [all_bits[0], all_bits[1], all_bits[3]]
    far_bits = [all_bits[2], all_bits[4], all_bits[5]]
    own_block = exchange_sum(scatter_sum(packed, near_bits), far_bits)
    own_block = own_block.reshape(all_tokens, -1, block + 1)
    inv_attn = lax.rsqrt(own_block[:, 0, block] / model_width + EPSILON)
    own_qkv = (inv_attn[:, None, None] * own_block[:, :, :block]).astype(jnp.bfloat16)
    qkv = gather_cols(own_qkv.reshape(all_tokens, -1), bits=near_bits)
    own_lengths = jnp.broadcast_to(private_lengths[:, None], (requests, NEW)).reshape(all_tokens)
    places = (
        prefix_block * lax.axis_size("tp")
        + own_lengths
        + jnp.arange(all_tokens, dtype=jnp.int32) % NEW
    )
    queries = rotate_heads(
        qkv[:, :model_width].astype(jnp.float32).reshape(all_tokens, HEADS, HDIM), places
    ).astype(jnp.bfloat16)
    fresh_keys = rotate_heads(
        qkv[:, model_width : 2 * model_width].astype(jnp.float32).reshape(all_tokens, HEADS, HDIM),
        places,
    ).astype(jnp.bfloat16)
    fresh_values = qkv[:, 2 * model_width :].astype(jnp.float32).reshape(requests, NEW, HEADS, HDIM)
    query_f = queries.astype(jnp.float32).reshape(requests, NEW, HEADS, HDIM)
    query_b = queries.reshape(requests, NEW, HEADS, HDIM)
    pre_keys = prefix_keys.reshape(group_count, prefix_block, HEADS, HDIM)
    pre_scores = (
        jnp.einsum("rjhd,gphd->rjhgp", query_b, pre_keys, preferred_element_type=jnp.float32)
        * score_scale
    )
    member = group_ids[:, None] == jnp.arange(group_count, dtype=jnp.int32)[None, :]
    pre_scores = jnp.where(member[:, None, None, :, None], pre_scores, BLOCKED)
    priv_keys = private_keys.reshape(requests, private_block, HEADS, HDIM)
    priv_scores = (
        jnp.einsum("rjhd,rphd->rjhp", query_b, priv_keys, preferred_element_type=jnp.float32)
        * score_scale
    )
    slots = own_rank * private_block + jnp.arange(private_block, dtype=jnp.int32)
    live = slots[None, :] < private_lengths[:, None]
    priv_scores = jnp.where(live[:, None, None, :], priv_scores, BLOCKED)
    local_peak = jnp.maximum(jnp.max(pre_scores, axis=(3, 4)), jnp.max(priv_scores, axis=3))
    pre_weights = jnp.exp(pre_scores - local_peak[..., None, None])
    priv_weights = jnp.exp(priv_scores - local_peak[..., None])
    local_total = jnp.sum(pre_weights, axis=(3, 4)) + jnp.sum(priv_weights, axis=3)
    pre_vals = prefix_values.astype(jnp.float32).reshape(group_count, prefix_block, HEADS, HDIM)
    priv_vals = private_values.astype(jnp.float32).reshape(requests, private_block, HEADS, HDIM)
    local_weighted = jnp.einsum("rjhgp,gphd->rjhd", pre_weights, pre_vals) + jnp.einsum(
        "rjhp,rphd->rjhd", priv_weights, priv_vals
    )
    local_peak = local_peak.reshape(all_tokens, HEADS)
    local_total = local_total.reshape(all_tokens, HEADS)
    local_weighted = local_weighted.reshape(all_tokens, model_width)
    cache_rows = scatter_merge(state_rows(local_peak, local_total, local_weighted), near_bits)
    cache_rows = exchange_merge(cache_rows, far_bits)
    key_f = fresh_keys.astype(jnp.float32).reshape(requests, NEW, HEADS, HDIM)
    new_scores = jnp.einsum("rjhd,rihd->rjhi", query_f, key_f) * score_scale
    causal = jnp.arange(NEW)[:, None] >= jnp.arange(NEW)[None, :]
    new_scores = jnp.where(causal[None, :, None, :], new_scores, BLOCKED)
    new_peak = jnp.max(new_scores, axis=3)
    new_weights = jnp.exp(new_scores - new_peak[..., None])
    new_total = jnp.sum(new_weights, axis=3).reshape(all_tokens, HEADS)
    new_weighted = jnp.einsum("rjhi,rihd->rjhd", new_weights, fresh_values).reshape(
        all_tokens, model_width
    )
    new_peak = new_peak.reshape(all_tokens, HEADS)
    new_rows = state_rows(new_peak, new_total, new_weighted)
    own_count = cache_rows.shape[0]
    new_rows = lax.dynamic_slice_in_dim(new_rows, kept_position(near_bits) * own_count, own_count, axis=0)
    final_rows = merge_rows(cache_rows, new_rows)
    attended_rows = (final_rows[:, :HDIM] / final_rows[:, HDIM : HDIM + 1]).astype(jnp.bfloat16)
    attended_lines = attended_rows.reshape(attended_rows.shape[0] // 2, 2 * HDIM)
    attended = gather_cols(attended_lines, axis=0, bits=near_bits).reshape(all_tokens, model_width)
    residual_cols = hidden + jnp.dot(attended, w_out, preferred_element_type=jnp.float32)
    full_rows = exchange_gather(residual_cols.astype(jnp.bfloat16)).astype(jnp.float32)
    inv_norm = lax.rsqrt(jnp.mean(full_rows * full_rows, axis=1) + EPSILON)
    normed = (full_rows * inv_norm[:, None] * moe_gain[None, :]).astype(jnp.bfloat16)
    logits = jnp.dot(normed, router, preferred_element_type=jnp.float32)
    expert_ids = jnp.arange(logits.shape[1], dtype=jnp.int32)
    first_pick = routes[:, 0:1] == expert_ids[None, :]
    second_pick = routes[:, 1:2] == expert_ids[None, :]
    first_logit = jnp.sum(jnp.where(first_pick, logits, 0.0), axis=1)
    second_logit = jnp.sum(jnp.where(second_pick, logits, 0.0), axis=1)
    first_weight = jax.nn.sigmoid(first_logit - second_logit)
    unit_count = w_gate.shape[1]
    own_expert = own_rank * unit_count // FF
    mix_coef = first_weight * (routes[:, 0] == own_expert).astype(jnp.float32) + (
        1.0 - first_weight
    ) * (routes[:, 1] == own_expert).astype(jnp.float32)
    gate_out = jnp.dot(normed, w_gate, preferred_element_type=jnp.float32)
    up_out = jnp.dot(normed, w_up, preferred_element_type=jnp.float32)
    inner_act = (jax.nn.silu(gate_out) * up_out * mix_coef[:, None]).astype(jnp.bfloat16)
    expert_blocks = jnp.einsum(
        "tf,fbc->btc",
        inner_act,
        w_down.reshape(w_down.shape[0], tp_count, -1),
        preferred_element_type=jnp.float32,
    )
    return residual_cols + exchange_scatter_sum(expert_blocks.astype(jnp.bfloat16))


def solution(mesh):
    placed = (
        P("rep", "tp"),
        P("tp"),
        P("tp", None),
        P(None, "tp"),
        P("rep", "tp", None),
        P("rep", "tp", None),
        P("rep", "tp", None),
        P("rep", "tp", None),
        P("rep"),
        P("rep"),
        P(),
        P(),
        P(None, "tp"),
        P(None, "tp"),
        P("tp", None),
        P("rep", None),
    )
    return jax.shard_map(
        on_device, mesh=mesh, in_specs=placed, out_specs=P("rep", "tp"), check_vma=False
    )
```

```python
import jax
import jax.numpy as jnp
from jax import lax
from jax.sharding import PartitionSpec as P

HEADS = 36
HDIM = 64
FF = 2880
NEW = 4


EPSILON = 1e-05
BLOCKED = -1e30


def rotate_heads(vectors, places):
    half_dim = HDIM // 2
    frequencies = 10000.0 ** (-jnp.arange(half_dim, dtype=jnp.float32) / half_dim)
    angles = places.astype(jnp.float32)[:, None] * frequencies[None, :]
    cosine = jnp.cos(angles)[:, None, :]
    sine_part = jnp.sin(angles)[:, None, :]
    first = vectors[..., :half_dim]
    second = vectors[..., half_dim:]
    return jnp.concatenate(
        [first * cosine - second * sine_part, second * cosine + first * sine_part], axis=-1
    )


def scale_rows(values, factor):
    row_count, head_count = factor.shape
    return (values.reshape(row_count, head_count, -1) * factor[..., None]).reshape(row_count, -1)


def partner_pairs(count, bit):
    return [(i, i ^ bit) for i in range(count)]


def tp_bits():
    count = lax.axis_size("tp")
    bits = []
    bit = 1
    while bit < count:
        bits.append(bit)
        bit *= 2
    return count, bits


def scatter_sum(values, bits=None):
    count, all_bits = tp_bits()
    bits = all_bits if bits is None else bits
    own_rank = lax.axis_index("tp")
    for bit in bits:
        half = values.shape[1] // 2
        side = (own_rank // bit) % 2
        keep = lax.dynamic_slice_in_dim(values, side * half, half, axis=1)
        send = lax.dynamic_slice_in_dim(values, (1 - side) * half, half, axis=1)
        values = keep + lax.ppermute(send, "tp", partner_pairs(count, bit))
    return values


def gather_cols(values, axis=1, bits=None):
    count, all_bits = tp_bits()
    bits = all_bits if bits is None else bits
    own_rank = lax.axis_index("tp")
    for bit in reversed(bits):
        side = (own_rank // bit) % 2
        other = lax.ppermute(values, "tp", partner_pairs(count, bit))
        values = jnp.where(
            side == 0,
            jnp.concatenate([values, other], axis=axis),
            jnp.concatenate([other, values], axis=axis),
        )
    return values


def kept_position(bits):
    own_rank = lax.axis_index("tp")
    position = 0
    for level, bit in enumerate(bits):
        position = position + ((own_rank // bit) % 2) * 2 ** (len(bits) - 1 - level)
    return position


def exchange_sum(values, bits):
    count, _ = tp_bits()
    for bit in bits:
        values = values + lax.ppermute(values, "tp", partner_pairs(count, bit))
    return values


def exchange_merge(rows, bits):
    count, _ = tp_bits()
    for bit in bits:
        rows = merge_rows(rows, lax.ppermute(rows, "tp", partner_pairs(count, bit)))
    return rows


def merge_rows(first, second):
    joint = jnp.maximum(first[:, -1:], second[:, -1:])
    first_factor = jnp.exp(first[:, -1:] - joint)
    second_factor = jnp.exp(second[:, -1:] - joint)
    body = first[:, :-1] * first_factor + second[:, :-1] * second_factor
    return jnp.concatenate([body, joint], axis=1)


def scatter_merge(rows, bits):
    count, _ = tp_bits()
    own_rank = lax.axis_index("tp")
    for bit in bits:
        half = rows.shape[0] // 2
        side = (own_rank // bit) % 2
        keep = lax.dynamic_slice_in_dim(rows, side * half, half, axis=0)
        send = lax.dynamic_slice_in_dim(rows, (1 - side) * half, half, axis=0)
        rows = merge_rows(keep, lax.ppermute(send, "tp", partner_pairs(count, bit)))
    return rows


def state_rows(peak, total, weighted):
    row_count = peak.shape[0] * peak.shape[1]
    return jnp.concatenate(
        [weighted.reshape(row_count, -1), total.reshape(row_count, 1), peak.reshape(row_count, 1)],
        axis=1,
    )


def exchange_gather(values):
    count = lax.axis_size("tp")
    copies = jnp.broadcast_to(values[None], (count,) + values.shape)
    received = lax.all_to_all(copies, "tp", 0, 0, tiled=True)
    return jnp.transpose(received, (1, 0, 2)).reshape(values.shape[0], -1)


def exchange_scatter_sum(blocks):
    received = lax.all_to_all(blocks, "tp", 0, 0, tiled=True)
    return jnp.sum(received.astype(jnp.float32), axis=0)


def reverse_blocks(values, count):
    rows, width = values.shape
    levels = count.bit_length() - 1
    split = values.reshape((rows,) + (2,) * levels + (width // count,))
    order = (0,) + tuple(range(levels, 0, -1)) + (levels + 1,)
    return split.transpose(order).reshape(rows, width)


def on_device(
    hidden,
    attn_gain,
    w_qkv,
    w_out,
    prefix_keys,
    prefix_values,
    private_keys,
    private_values,
    group_ids,
    private_lengths,
    moe_gain,
    router,
    w_gate,
    w_up,
    w_down,
    routes,
):
    model_width = w_out.shape[0]
    all_tokens = hidden.shape[0]
    requests = group_ids.shape[0]
    group_count = prefix_keys.shape[0]
    prefix_block = prefix_keys.shape[1]
    private_block = private_keys.shape[1]
    own_rank = lax.axis_index("tp")
    score_scale = HDIM ** (-0.5)
    scaled = (hidden * attn_gain[None, :]).astype(jnp.bfloat16)
    partial_qkv = jnp.dot(scaled, w_qkv, preferred_element_type=jnp.float32)
    own_squares = jnp.sum(hidden * hidden, axis=1)
    qkv_width = partial_qkv.shape[1]
    tp_count = lax.axis_size("tp")
    block = qkv_width // tp_count
    packed = jnp.concatenate(
        [
            partial_qkv.reshape(all_tokens, tp_count, block),
            jnp.broadcast_to(own_squares[:, None, None], (all_tokens, tp_count, 1)),
        ],
        axis=2,
    ).reshape(all_tokens, tp_count * (block + 1))
    _, all_bits = tp_bits()
    near_bits = [all_bits[0], all_bits[3], all_bits[1]]
    far_bits = [all_bits[2], all_bits[4], all_bits[5]]
    own_block = exchange_sum(scatter_sum(packed, near_bits), far_bits)
    own_block = own_block.reshape(all_tokens, -1, block + 1)
    inv_attn = lax.rsqrt(own_block[:, 0, block] / model_width + EPSILON)
    own_qkv = (inv_attn[:, None, None] * own_block[:, :, :block]).astype(jnp.bfloat16)
    qkv = gather_cols(own_qkv.reshape(all_tokens, -1), bits=near_bits)
    own_lengths = jnp.broadcast_to(private_lengths[:, None], (requests, NEW)).reshape(all_tokens)
    places = (
        prefix_block * lax.axis_size("tp")
        + own_lengths
        + jnp.arange(all_tokens, dtype=jnp.int32) % NEW
    )
    queries = rotate_heads(
        qkv[:, :model_width].astype(jnp.float32).reshape(all_tokens, HEADS, HDIM), places
    ).astype(jnp.bfloat16)
    fresh_keys = rotate_heads(
        qkv[:, model_width : 2 * model_width].astype(jnp.float32).reshape(all_tokens, HEADS, HDIM),
        places,
    ).astype(jnp.bfloat16)
    fresh_values = qkv[:, 2 * model_width :].astype(jnp.float32).reshape(requests, NEW, HEADS, HDIM)
    query_f = queries.astype(jnp.float32).reshape(requests, NEW, HEADS, HDIM)
    query_b = queries.reshape(requests, NEW, HEADS, HDIM)
    pre_keys = prefix_keys.reshape(group_count, prefix_block, HEADS, HDIM)
    pre_scores = (
        jnp.einsum("rjhd,gphd->rjhgp", query_b, pre_keys, preferred_element_type=jnp.float32)
        * score_scale
    )
    member = group_ids[:, None] == jnp.arange(group_count, dtype=jnp.int32)[None, :]
    pre_scores = jnp.where(member[:, None, None, :, None], pre_scores, BLOCKED)
    priv_keys = private_keys.reshape(requests, private_block, HEADS, HDIM)
    priv_scores = (
        jnp.einsum("rjhd,rphd->rjhp", query_b, priv_keys, preferred_element_type=jnp.float32)
        * score_scale
    )
    slots = own_rank * private_block + jnp.arange(private_block, dtype=jnp.int32)
    live = slots[None, :] < private_lengths[:, None]
    priv_scores = jnp.where(live[:, None, None, :], priv_scores, BLOCKED)
    local_peak = jnp.maximum(jnp.max(pre_scores, axis=(3, 4)), jnp.max(priv_scores, axis=3))
    pre_weights = jnp.exp(pre_scores - local_peak[..., None, None])
    priv_weights = jnp.exp(priv_scores - local_peak[..., None])
    local_total = jnp.sum(pre_weights, axis=(3, 4)) + jnp.sum(priv_weights, axis=3)
    pre_vals = prefix_values.astype(jnp.float32).reshape(group_count, prefix_block, HEADS, HDIM)
    priv_vals = private_values.astype(jnp.float32).reshape(requests, private_block, HEADS, HDIM)
    local_weighted = jnp.einsum("rjhgp,gphd->rjhd", pre_weights, pre_vals) + jnp.einsum(
        "rjhp,rphd->rjhd", priv_weights, priv_vals
    )
    local_peak = local_peak.reshape(all_tokens, HEADS)
    local_total = local_total.reshape(all_tokens, HEADS)
    local_weighted = local_weighted.reshape(all_tokens, model_width)
    cache_rows = scatter_merge(state_rows(local_peak, local_total, local_weighted), near_bits)
    cache_rows = exchange_merge(cache_rows, far_bits)
    key_f = fresh_keys.astype(jnp.float32).reshape(requests, NEW, HEADS, HDIM)
    new_scores = jnp.einsum("rjhd,rihd->rjhi", query_f, key_f) * score_scale
    causal = jnp.arange(NEW)[:, None] >= jnp.arange(NEW)[None, :]
    new_scores = jnp.where(causal[None, :, None, :], new_scores, BLOCKED)
    new_peak = jnp.max(new_scores, axis=3)
    new_weights = jnp.exp(new_scores - new_peak[..., None])
    new_total = jnp.sum(new_weights, axis=3).reshape(all_tokens, HEADS)
    new_weighted = jnp.einsum("rjhi,rihd->rjhd", new_weights, fresh_values).reshape(
        all_tokens, model_width
    )
    new_peak = new_peak.reshape(all_tokens, HEADS)
    new_rows = state_rows(new_peak, new_total, new_weighted)
    own_count = cache_rows.shape[0]
    new_rows = lax.dynamic_slice_in_dim(new_rows, kept_position(near_bits) * own_count, own_count, axis=0)
    final_rows = merge_rows(cache_rows, new_rows)
    attended_rows = (final_rows[:, :HDIM] / final_rows[:, HDIM : HDIM + 1]).astype(jnp.bfloat16)
    attended_lines = attended_rows.reshape(attended_rows.shape[0] // 2, 2 * HDIM)
    attended = gather_cols(attended_lines, axis=0, bits=near_bits).reshape(all_tokens, model_width)
    residual_cols = hidden + jnp.dot(attended, w_out, preferred_element_type=jnp.float32)
    full_rows = exchange_gather(residual_cols.astype(jnp.bfloat16)).astype(jnp.float32)
    inv_norm = lax.rsqrt(jnp.mean(full_rows * full_rows, axis=1) + EPSILON)
    normed = (full_rows * inv_norm[:, None] * moe_gain[None, :]).astype(jnp.bfloat16)
    logits = jnp.dot(normed, router, preferred_element_type=jnp.float32)
    expert_ids = jnp.arange(logits.shape[1], dtype=jnp.int32)
    first_pick = routes[:, 0:1] == expert_ids[None, :]
    second_pick = routes[:, 1:2] == expert_ids[None, :]
    first_logit = jnp.sum(jnp.where(first_pick, logits, 0.0), axis=1)
    second_logit = jnp.sum(jnp.where(second_pick, logits, 0.0), axis=1)
    first_weight = jax.nn.sigmoid(first_logit - second_logit)
    unit_count = w_gate.shape[1]
    own_expert = own_rank * unit_count // FF
    mix_coef = first_weight * (routes[:, 0] == own_expert).astype(jnp.float32) + (
        1.0 - first_weight
    ) * (routes[:, 1] == own_expert).astype(jnp.float32)
    gate_out = jnp.dot(normed, w_gate, preferred_element_type=jnp.float32)
    up_out = jnp.dot(normed, w_up, preferred_element_type=jnp.float32)
    inner_act = (jax.nn.silu(gate_out) * up_out * mix_coef[:, None]).astype(jnp.bfloat16)
    expert_blocks = jnp.einsum(
        "tf,fbc->btc",
        inner_act,
        w_down.reshape(w_down.shape[0], tp_count, -1),
        preferred_element_type=jnp.float32,
    )
    return residual_cols + exchange_scatter_sum(expert_blocks.astype(jnp.bfloat16))


def solution(mesh):
    placed = (
        P("rep", "tp"),
        P("tp"),
        P("tp", None),
        P(None, "tp"),
        P("rep", "tp", None),
        P("rep", "tp", None),
        P("rep", "tp", None),
        P("rep", "tp", None),
        P("rep"),
        P("rep"),
        P(),
        P(),
        P(None, "tp"),
        P(None, "tp"),
        P("tp", None),
        P("rep", None),
    )
    return jax.shard_map(
        on_device, mesh=mesh, in_specs=placed, out_specs=P("rep", "tp"), check_vma=False
    )
```
